32 devices in a mesh: grp: 2 (over x), tm: 16 (over z, y, core).
Axes of the slice: x: 2, y: 2, z: 4, core: 2. Of those that a mesh axis runs over, the one named last changes fastest.
Arguments:
- signals: bfloat16 [8, 1024, 256], P('grp', 'tm'), parts along dimension 0, may hold values from -6 to 6
- targets: bfloat16 [8, 1024, 768], P('grp', 'tm'), parts along dimension 0, may hold values from -6 to 6
- decay_rate: float32 [4096], P('grp'), parts along dimension 0, may hold values from 0 to 0.125, as said below
- pole_angle: float32 [4096], P('grp'), parts along dimension 0, may hold values from -3.1416 to 3.1416
- in_map: bfloat16 [8192, 256], P('grp'), parts along dimension 0
- out_map: bfloat16 [8192, 768], P('grp'), parts along dimension 0
Outputs:
- out_update: float32 [8192, 768], P(('grp', 'tm')), parts along dimension 0
- in_update: float32 [8192, 256], P(('grp', 'tm')), parts along dimension 0
- boundary_adjoint: float32 [8, 16, 4096], P('grp', 'tm'), parts along dimension 0
The draws below stay inside these ranges and needn't reach their ends.
There are 2 independent parts, one for each index of `grp`. The reference program is written for one: setup_inputs(seed, part) draws one part's arguments, and reference() takes and returns one part's arrays. A program takes and returns all parts, laid end to end along the dimension named above; each array names one. Nothing has to cross between parts.
Inputs may be any that keep to these rules, and one draw needn't show every extreme that they name: Every mode decays: exp(-decay_rate) lies below 1.
All inputs are finite; a program needn't handle non-finite values.
Results may differ from the reference program's by a relative error of at most 0.0027.
Values sent between devices are 32-bit elements; how exact they have to be, the bound alone decides.
No kernel may reach another device: no remote copies, remote signals or barrier semaphores. Data moves between devices by JAX's collectives and lax.ppermute only.
A program may use at most 128 MiB of HBM per device.

```python
import math
import jax
import jax.numpy as jnp
from jax import lax

MODES = 2048
SENSORS = 256
TARGETS = 768
MEMBERS = 4
GROUP = 64
STEPS = 1024
N_TM = 16


def mode_draws(key):
    keys = jax.random.split(jax.random.fold_in(key, 101), 7)
    slow_share = 0.4
    mid_share = 0.35
    pick = jax.random.uniform(keys[0], (MODES,), jnp.float32)
    slow_rate = jnp.exp(jax.random.uniform(keys[1], (MODES,), jnp.float32, math.log(0.05), math.log(2.0))) / STEPS
    mid_rate = 1.0 / jax.random.uniform(keys[2], (MODES,), jnp.float32, 52.0, 63.5)
    fast_rate = 1.0 / jax.random.uniform(keys[3], (MODES,), jnp.float32, 8.0, 40.0)
    rate = jnp.where(pick < slow_share, slow_rate, jnp.where(pick < slow_share + mid_share, mid_rate, fast_rate))
    still = jax.random.uniform(keys[4], (MODES,), jnp.float32) < 0.5
    small_turn = rate * jax.random.uniform(keys[5], (MODES,), jnp.float32, -0.3, 0.3)
    full_turn = jax.random.uniform(keys[6], (MODES,), jnp.float32, -math.pi, math.pi)
    turn = jnp.where(still, small_turn, full_turn)
    return (rate.astype(jnp.float32), turn.astype(jnp.float32))


def draw_decay_rate(key, part):
    rate, turn = mode_draws(key)
    return rate


def draw_pole_angle(key, part):
    rate, turn = mode_draws(key)
    return turn


def map_draw(key, salt, height, breadth, fan):
    keys = jax.random.split(jax.random.fold_in(key, salt), 3)
    base = jnp.clip(jax.random.normal(keys[0], (height, breadth), jnp.float32), -6.0, 6.0)
    row_scale = jnp.exp(jax.random.uniform(keys[1], (height, 1), jnp.float32, math.log(0.35), math.log(2.8)))
    imag_scale = jnp.exp(jax.random.uniform(keys[2], (), jnp.float32, math.log(0.15), math.log(0.35)))
    side = jnp.where(jnp.arange(height)[:, None] >= MODES, imag_scale, jnp.float32(1.0))
    return (base * row_scale * side * float(fan) ** (-0.5)).astype(jnp.float32)


def draw_in_map(key, part):
    return map_draw(key, 211, 2 * MODES, SENSORS, SENSORS).astype(jnp.bfloat16)


def draw_out_map(key, part):
    return map_draw(key, 307, 2 * MODES, TARGETS, 2 * MODES).astype(jnp.bfloat16)


def levels(key, extent, cuts, smallest, largest):
    loudness = 1.0
    for position, blocks in cuts:
        draws = jax.random.uniform(jax.random.fold_in(jax.random.fold_in(key, 6), position), (blocks,), jnp.float32, smallest / len(cuts), largest / len(cuts))
        loudness = loudness * jnp.repeat(jnp.exp(draws), extent[position] // blocks).reshape((-1,) + (1,) * (len(extent) - 1 - position))
    return loudness


def normal_values(rng, shape, width, reach, cuts=(), held_as=jnp.bfloat16):
    result = width * jax.random.normal(rng, shape, jnp.float32)
    if cuts:
        result = result * levels(rng, shape, cuts, -0.22, 0.18)
    return jnp.clip(result, -reach, reach).astype(held_as)


def setup_inputs(seed: int = 0, part: int = 0) -> dict:
    streams_of = jax.random.split(jax.random.key(seed), 7)
    part_keys = jax.random.split(jax.random.fold_in(streams_of[6], part), 7)
    return {
        "signals": normal_values(part_keys[0], (MEMBERS, STEPS, SENSORS), 1.0, 6.0, ((1, 16),)),
        "targets": normal_values(part_keys[1], (MEMBERS, STEPS, TARGETS), 1.0, 6.0, ((1, 16),)),
        "decay_rate": draw_decay_rate(jax.random.fold_in(jax.random.fold_in(streams_of[6], part), 71), part),
        "pole_angle": draw_pole_angle(jax.random.fold_in(jax.random.fold_in(streams_of[6], part), 71), part),
        "in_map": draw_in_map(jax.random.fold_in(jax.random.fold_in(streams_of[6], part), 71), part),
        "out_map": draw_out_map(jax.random.fold_in(jax.random.fold_in(streams_of[6], part), 71), part),
    }


def cmul(first, second):
    half = first.shape[-1] // 2
    fr = first[..., :half]
    fi = first[..., half:]
    sr = second[..., :half]
    si = second[..., half:]
    return jnp.concatenate([fr * sr - fi * si, fr * si + fi * sr], axis=-1)

def reference(signals, targets, decay_rate, pole_angle, in_map, out_map):
    magnitude = jnp.exp(-decay_rate)
    step_pair = jnp.concatenate([magnitude * jnp.cos(pole_angle), magnitude * jnp.sin(pole_angle)])
    conj_pair = jnp.concatenate([magnitude * jnp.cos(pole_angle), -magnitude * jnp.sin(pole_angle)])
    gain = jnp.sqrt(-jnp.expm1(-2.0 * decay_rate))
    gain_pair = jnp.concatenate([gain, gain])
    sig_blocks = signals.reshape(MEMBERS, N_TM, GROUP, SENSORS).transpose(1, 0, 2, 3)
    tgt_blocks = targets.reshape(MEMBERS, N_TM, GROUP, TARGETS).transpose(1, 0, 2, 3)

    def forward(carry, block):
        state, grad_out = carry
        sig, tgt = block
        drive = lax.dot_general(sig, in_map, (((2,), (1,)), ((), ())), preferred_element_type=jnp.float32) * gain_pair

        def advance(current, column):
            following = cmul(step_pair, current) + column
            return (following, following)
        state, seq = lax.scan(advance, state, drive.transpose(1, 0, 2))
        states_b = seq.transpose(1, 0, 2).astype(jnp.bfloat16)
        predicted = lax.dot_general(states_b, out_map, (((2,), (0,)), ((), ())), preferred_element_type=jnp.float32)
        misfit_b = (predicted - tgt.astype(jnp.float32)).astype(jnp.bfloat16)
        grad_out = grad_out + lax.dot_general(states_b, misfit_b, (((0, 1), (0, 1)), ((), ())), preferred_element_type=jnp.float32)
        return ((state, grad_out), misfit_b)
    start_state = jnp.zeros((MEMBERS, 2 * MODES), jnp.float32)
    start_out = jnp.zeros((2 * MODES, TARGETS), jnp.float32)
    (last_state, grad_out), misfits = lax.scan(forward, (start_state, start_out), (sig_blocks, tgt_blocks))

    def backward(carry, block):
        adjoint, grad_in = carry
        sig, misfit_b = block
        back = lax.dot_general(misfit_b, out_map, (((2,), (1,)), ((), ())), preferred_element_type=jnp.float32)

        def retreat(later, column):
            present = cmul(conj_pair, later) + column
            return (present, present)
        adjoint, seq = lax.scan(retreat, adjoint, back.transpose(1, 0, 2), reverse=True)
        scaled = seq.transpose(1, 0, 2) * gain_pair
        adjoint_b = scaled.astype(jnp.bfloat16)
        grad_in = grad_in + lax.dot_general(adjoint_b, sig, (((0, 1), (0, 1)), ((), ())), preferred_element_type=jnp.float32)
        return ((adjoint, grad_in), scaled[:, 0])
    start_in = jnp.zeros((2 * MODES, SENSORS), jnp.float32)
    (last_adjoint, grad_in), firsts = lax.scan(backward, (start_state, start_in), (sig_blocks, misfits), reverse=True)
    out_update = grad_out / jnp.sqrt(jnp.mean(grad_out * grad_out) + 1e-06)
    in_update = grad_in / jnp.sqrt(jnp.mean(grad_in * grad_in) + 1e-06)
    boundary_adjoint = firsts.transpose(1, 0, 2)
    return (out_update, in_update, boundary_adjoint)
```

```python
import math

import jax
import jax.numpy as jnp
from jax import lax
from jax.sharding import PartitionSpec as P


def cmul(first, second):
    half = first.shape[-1] // 2
    fr = first[..., :half]
    fi = first[..., half:]
    sr = second[..., :half]
    si = second[..., half:]
    return jnp.concatenate([fr * sr - fi * si, fr * si + fi * sr], axis=-1)


def mode_powers(decay_rate, angle, unit, counts):
    phase = jnp.mod(angle * unit, 2.0 * math.pi) * counts
    magnitude = jnp.exp(-decay_rate * unit * counts)
    return jnp.concatenate([magnitude * jnp.cos(phase), magnitude * jnp.sin(phase)], axis=-1)


def carry_in(values, rate_row, angle_row, group, count, reverse):
    unit_one = jnp.ones((1, 1), jnp.float32)

    def pairs(span):
        if reverse:
            return [(i + span, i) for i in range(count - span)]
        return [(i, i + span) for i in range(count - span)]

    if count == 1:
        return jnp.zeros_like(values)
    acc = lax.ppermute(values, "tm", pairs(1))
    span = 1
    while span < count:
        factor = mode_powers(rate_row, angle_row, float(group * span), unit_one)
        acc = acc + cmul(factor, lax.ppermute(acc, "tm", pairs(span)))
        span = span * 2
    return acc


def tm_sum(value, count):
    if count & (count - 1):
        return lax.psum(value, "tm")
    span = 1
    while span < count:
        value = value + lax.ppermute(value, "tm", [(i, i ^ span) for i in range(count)])
        span = span * 2
    return value


def per_device(signals, targets, decay_rate, pole_angle, in_map, out_map):
    group = signals.shape[1]
    modes = decay_rate.shape[0]
    width = 2 * modes
    count = lax.axis_size("tm")
    rate_row = decay_rate[None, :]
    fwd_angle = pole_angle[None, :]
    rev_angle = -pole_angle[None, :]
    gain = jnp.sqrt(-jnp.expm1(-2.0 * decay_rate))
    gain_pair = jnp.concatenate([gain, gain])
    unit_one = jnp.ones((1, 1), jnp.float32)
    drive = (
        lax.dot_general(
            signals, in_map, (((2,), (1,)), ((), ())), preferred_element_type=jnp.float32
        )
        * gain_pair
    )
    local = drive
    span = 1
    while span < group:
        factor = mode_powers(rate_row, fwd_angle, float(span), unit_one)
        local = jnp.concatenate(
            [local[:, :span], local[:, span:] + cmul(factor[None], local[:, :-span])], axis=1
        )
        span = span * 2
    ends = local[:, group - 1]
    entering = carry_in(ends, rate_row, fwd_angle, group, count, False)
    offsets = (jnp.arange(group, dtype=jnp.float32) + 1.0)[:, None]
    fwd_table = mode_powers(rate_row, fwd_angle, 1.0, offsets)
    states = local + cmul(fwd_table[None], entering[:, None, :])
    states_b = states.astype(jnp.bfloat16)
    predicted = lax.dot_general(
        states_b, out_map, (((2,), (0,)), ((), ())), preferred_element_type=jnp.float32
    )
    misfit_b = (predicted - targets.astype(jnp.float32)).astype(jnp.bfloat16)
    back = lax.dot_general(
        misfit_b, out_map, (((2,), (1,)), ((), ())), preferred_element_type=jnp.float32
    )
    retro = back
    span = 1
    while span < group:
        factor = mode_powers(rate_row, rev_angle, float(span), unit_one)
        retro = jnp.concatenate(
            [retro[:, :-span] + cmul(factor[None], retro[:, span:]), retro[:, group - span :]],
            axis=1,
        )
        span = span * 2
    starts = retro[:, 0]
    later = carry_in(starts, rate_row, rev_angle, group, count, True)
    remaining = (float(group) - jnp.arange(group, dtype=jnp.float32))[:, None]
    rev_table = mode_powers(rate_row, rev_angle, 1.0, remaining)
    adjoint = retro + cmul(rev_table[None], later[:, None, :])
    scaled = adjoint * gain_pair
    adjoint_b = scaled.astype(jnp.bfloat16)
    boundary_adjoint = scaled[:, 0:1, :]
    out_grad = lax.psum_scatter(
        lax.dot_general(
            states_b, misfit_b, (((0, 1), (0, 1)), ((), ())), preferred_element_type=jnp.float32
        ),
        "tm",
        scatter_dimension=0,
        tiled=True,
    )
    in_grad = lax.psum_scatter(
        lax.dot_general(
            adjoint_b, signals, (((0, 1), (0, 1)), ((), ())), preferred_element_type=jnp.float32
        ),
        "tm",
        scatter_dimension=0,
        tiled=True,
    )
    out_square = tm_sum(jnp.sum(out_grad * out_grad), count)
    out_update = out_grad * lax.rsqrt(out_square / float(width * out_map.shape[1]) + 1e-06)
    in_square = tm_sum(jnp.sum(in_grad * in_grad), count)
    in_update = in_grad * lax.rsqrt(in_square / float(width * in_map.shape[1]) + 1e-06)
    return (out_update, in_update, boundary_adjoint)


def solution(mesh):
    return jax.shard_map(
        per_device,
        mesh=mesh,
        in_specs=(
            P("grp", "tm", None),
            P("grp", "tm", None),
            P("grp"),
            P("grp"),
            P("grp", None),
            P("grp", None),
        ),
        out_specs=(P(("grp", "tm"), None), P(("grp", "tm"), None), P("grp", "tm", None)),
        check_vma=False,
    )
```

```python
import math

import jax
import jax.numpy as jnp
from jax import lax
from jax.sharding import PartitionSpec as P


def cmul(first, second):
    half = first.shape[-1] // 2
    fr = first[..., :half]
    fi = first[..., half:]
    sr = second[..., :half]
    si = second[..., half:]
    return jnp.concatenate([fr * sr - fi * si, fr * si + fi * sr], axis=-1)


def mode_powers(decay_rate, angle, unit, counts):
    phase = jnp.mod(angle * unit, 2.0 * math.pi) * counts
    magnitude = jnp.exp(-decay_rate * unit * counts)
    return jnp.concatenate([magnitude * jnp.cos(phase), magnitude * jnp.sin(phase)], axis=-1)


def carry_in(values, rate_row, angle_row, group, count, reverse):
    unit_one = jnp.ones((1, 1), jnp.float32)

    def pairs(span):
        if reverse:
            return [(i + span, i) for i in range(count - span)]
        return [(i, i + span) for i in range(count - span)]

    if count == 1:
        return jnp.zeros_like(values)
    acc = lax.ppermute(values, "tm", pairs(1))
    span = 1
    while span < count:
        factor = mode_powers(rate_row, angle_row, float(group * span), unit_one)
        acc = acc + cmul(factor, lax.ppermute(acc, "tm", pairs(span)))
        span = span * 2
    return acc


def tm_sum(value, count):
    if count & (count - 1):
        return lax.psum(value, "tm")
    span = 1
    while span < count:
        value = value + lax.ppermute(value, "tm", [(i, i ^ span) for i in range(count)])
        span = span * 2
    return value


def halving_scatter(value, count, order):
    depth = count.bit_length() - 1
    rows = value.shape[0] // count
    buf = value.reshape((2,) * depth + (rows, value.shape[1]))
    axes = list(range(depth - 1, -1, -1))
    index = lax.axis_index("tm")
    for bit in order:
        axis = axes.index(bit)
        mine = (index >> bit) & 1
        keep = lax.dynamic_index_in_dim(buf, mine, axis, keepdims=False)
        send = lax.dynamic_index_in_dim(buf, 1 - mine, axis, keepdims=False)
        buf = keep + lax.ppermute(send, "tm", [(i, i ^ (1 << bit)) for i in range(count)])
        axes.pop(axis)
    return buf.reshape(rows, value.shape[1])


def tm_scatter(value, count):
    if count & (count - 1) or count < 4:
        return lax.psum_scatter(value, "tm", scatter_dimension=0, tiled=True)
    depth = count.bit_length() - 1
    first = list(range(depth))
    second = [0, 2, 1] + list(range(3, depth))
    half = value.shape[1] // 2
    return jnp.concatenate(
        [
            halving_scatter(value[:, :half], count, first),
            halving_scatter(value[:, half:], count, second),
        ],
        axis=1,
    )


def per_device(signals, targets, decay_rate, pole_angle, in_map, out_map):
    group = signals.shape[1]
    modes = decay_rate.shape[0]
    width = 2 * modes
    count = lax.axis_size("tm")
    rate_row = decay_rate[None, :]
    fwd_angle = pole_angle[None, :]
    rev_angle = -pole_angle[None, :]
    gain = jnp.sqrt(-jnp.expm1(-2.0 * decay_rate))
    gain_pair = jnp.concatenate([gain, gain])
    unit_one = jnp.ones((1, 1), jnp.float32)
    drive = (
        lax.dot_general(
            signals, in_map, (((2,), (1,)), ((), ())), preferred_element_type=jnp.float32
        )
        * gain_pair
    )
    local = drive
    span = 1
    while span < group:
        factor = mode_powers(rate_row, fwd_angle, float(span), unit_one)
        local = jnp.concatenate(
            [local[:, :span], local[:, span:] + cmul(factor[None], local[:, :-span])], axis=1
        )
        span = span * 2
    ends = local[:, group - 1]
    entering = carry_in(ends, rate_row, fwd_angle, group, count, False)
    offsets = (jnp.arange(group, dtype=jnp.float32) + 1.0)[:, None]
    fwd_table = mode_powers(rate_row, fwd_angle, 1.0, offsets)
    states = local + cmul(fwd_table[None], entering[:, None, :])
    states_b = states.astype(jnp.bfloat16)
    predicted = lax.dot_general(
        states_b, out_map, (((2,), (0,)), ((), ())), preferred_element_type=jnp.float32
    )
    misfit_b = (predicted - targets.astype(jnp.float32)).astype(jnp.bfloat16)
    back = lax.dot_general(
        misfit_b, out_map, (((2,), (1,)), ((), ())), preferred_element_type=jnp.float32
    )
    retro = back
    span = 1
    while span < group:
        factor = mode_powers(rate_row, rev_angle, float(span), unit_one)
        retro = jnp.concatenate(
            [retro[:, :-span] + cmul(factor[None], retro[:, span:]), retro[:, group - span :]],
            axis=1,
        )
        span = span * 2
    starts = retro[:, 0]
    later = carry_in(starts, rate_row, rev_angle, group, count, True)
    remaining = (float(group) - jnp.arange(group, dtype=jnp.float32))[:, None]
    rev_table = mode_powers(rate_row, rev_angle, 1.0, remaining)
    adjoint = retro + cmul(rev_table[None], later[:, None, :])
    scaled = adjoint * gain_pair
    adjoint_b = scaled.astype(jnp.bfloat16)
    boundary_adjoint = scaled[:, 0:1, :]
    out_grad = tm_scatter(
        lax.dot_general(
            states_b, misfit_b, (((0, 1), (0, 1)), ((), ())), preferred_element_type=jnp.float32
        ),
        count,
    )
    in_grad = tm_scatter(
        lax.dot_general(
            adjoint_b, signals, (((0, 1), (0, 1)), ((), ())), preferred_element_type=jnp.float32
        ),
        count,
    )
    out_square = tm_sum(jnp.sum(out_grad * out_grad), count)
    out_update = out_grad * lax.rsqrt(out_square / float(width * out_map.shape[1]) + 1e-06)
    in_square = tm_sum(jnp.sum(in_grad * in_grad), count)
    in_update = in_grad * lax.rsqrt(in_square / float(width * in_map.shape[1]) + 1e-06)
    return (out_update, in_update, boundary_adjoint)


def solution(mesh):
    return jax.shard_map(
        per_device,
        mesh=mesh,
        in_specs=(
            P("grp", "tm", None),
            P("grp", "tm", None),
            P("grp"),
            P("grp"),
            P("grp", None),
            P("grp", None),
        ),
        out_specs=(P(("grp", "tm"), None), P(("grp", "tm"), None), P("grp", "tm", None)),
        check_vma=False,
    )
```

```python
import math

import jax
import jax.numpy as jnp
from jax import lax
from jax.sharding import PartitionSpec as P


def cmul(first, second):
    half = first.shape[-1] // 2
    fr = first[..., :half]
    fi = first[..., half:]
    sr = second[..., :half]
    si = second[..., half:]
    return jnp.concatenate([fr * sr - fi * si, fr * si + fi * sr], axis=-1)


def mode_powers(decay_rate, angle, unit, counts):
    phase = jnp.mod(angle * unit, 2.0 * math.pi) * counts
    magnitude = jnp.exp(-decay_rate * unit * counts)
    return jnp.concatenate([magnitude * jnp.cos(phase), magnitude * jnp.sin(phase)], axis=-1)


def radices(count):
    sizes = []
    left = count
    while left > 1:
        size = 4 if left % 4 == 0 else (2 if left % 2 == 0 else left)
        sizes.append(size)
        left = left // size
    return sizes


def carry_in(values, rate_row, angle_row, group, count, reverse):
    unit_one = jnp.ones((1, 1), jnp.float32)

    def shifted(source, span):
        if reverse:
            pairs = [(i + span, i) for i in range(count - span)]
        else:
            pairs = [(i, i + span) for i in range(count - span)]
        return lax.ppermute(source, "tm", pairs)

    if count == 1:
        return jnp.zeros_like(values)
    sizes = radices(count)
    first = min(sizes[0], count - 1)
    acc = shifted(values, 1)
    for step in range(2, first + 1):
        factor = mode_powers(rate_row, angle_row, float(group * (step - 1)), unit_one)
        acc = acc + cmul(factor, shifted(values, step))
    span = first
    for size in sizes[1:]:
        if span >= count - 1:
            break
        moved = acc
        for step in range(1, size):
            if step * span >= count:
                break
            factor = mode_powers(rate_row, angle_row, float(group * span * step), unit_one)
            moved = moved + cmul(factor, shifted(acc, step * span))
        acc = moved
        span = span * size
    return acc


def tm_sum(value, count):
    span = 1
    index = lax.axis_index("tm")
    for size in radices(count):
        if size > 4:
            return lax.psum(value, "tm")
        terms = [value]
        for offset in range(1, size):
            pairs = []
            for i in range(count):
                own = (i // span) % size
                source = i + ((own + offset) % size - own) * span
                pairs.append((source, i))
            terms.append(lax.ppermute(value, "tm", pairs))
        stack = jnp.stack(terms)
        mine = (index // span) % size
        total = None
        for digit in range(size):
            term = lax.dynamic_index_in_dim(stack, (digit - mine) % size, 0, keepdims=False)
            total = term if total is None else total + term
        value = total
        span = span * size
    return value


def halving_scatter(value, count, order):
    depth = count.bit_length() - 1
    rows = value.shape[0] // count
    buf = value.reshape((2,) * depth + (rows, value.shape[1]))
    axes = list(range(depth - 1, -1, -1))
    index = lax.axis_index("tm")
    for bit in order:
        axis = axes.index(bit)
        mine = (index >> bit) & 1
        keep = lax.dynamic_index_in_dim(buf, mine, axis, keepdims=False)
        send = lax.dynamic_index_in_dim(buf, 1 - mine, axis, keepdims=False)
        buf = keep + lax.ppermute(send, "tm", [(i, i ^ (1 << bit)) for i in range(count)])
        axes.pop(axis)
    return buf.reshape(rows, value.shape[1])


def tm_scatter(value, count):
    if count & (count - 1) or count < 4:
        return lax.psum_scatter(value, "tm", scatter_dimension=0, tiled=True)
    depth = count.bit_length() - 1
    first = list(range(depth))
    second = [0, 2, 1] + list(range(3, depth))
    half = value.shape[1] // 2
    return jnp.concatenate(
        [
            halving_scatter(value[:, :half], count, first),
            halving_scatter(value[:, half:], count, second),
        ],
        axis=1,
    )


def per_device(signals, targets, decay_rate, pole_angle, in_map, out_map):
    group = signals.shape[1]
    modes = decay_rate.shape[0]
    width = 2 * modes
    count = lax.axis_size("tm")
    rate_row = decay_rate[None, :]
    fwd_angle = pole_angle[None, :]
    rev_angle = -pole_angle[None, :]
    gain = jnp.sqrt(-jnp.expm1(-2.0 * decay_rate))
    gain_pair = jnp.concatenate([gain, gain])
    unit_one = jnp.ones((1, 1), jnp.float32)
    drive = (
        lax.dot_general(
            signals, in_map, (((2,), (1,)), ((), ())), preferred_element_type=jnp.float32
        )
        * gain_pair
    )
    local = drive
    span = 1
    while span < group:
        factor = mode_powers(rate_row, fwd_angle, float(span), unit_one)
        local = jnp.concatenate(
            [local[:, :span], local[:, span:] + cmul(factor[None], local[:, :-span])], axis=1
        )
        span = span * 2
    ends = local[:, group - 1]
    entering = carry_in(ends, rate_row, fwd_angle, group, count, False)
    offsets = (jnp.arange(group, dtype=jnp.float32) + 1.0)[:, None]
    fwd_table = mode_powers(rate_row, fwd_angle, 1.0, offsets)
    states = local + cmul(fwd_table[None], entering[:, None, :])
    states_b = states.astype(jnp.bfloat16)
    predicted = lax.dot_general(
        states_b, out_map, (((2,), (0,)), ((), ())), preferred_element_type=jnp.float32
    )
    misfit_b = (predicted - targets.astype(jnp.float32)).astype(jnp.bfloat16)
    back = lax.dot_general(
        misfit_b, out_map, (((2,), (1,)), ((), ())), preferred_element_type=jnp.float32
    )
    retro = back
    span = 1
    while span < group:
        factor = mode_powers(rate_row, rev_angle, float(span), unit_one)
        retro = jnp.concatenate(
            [retro[:, :-span] + cmul(factor[None], retro[:, span:]), retro[:, group - span :]],
            axis=1,
        )
        span = span * 2
    starts = retro[:, 0]
    later = carry_in(starts, rate_row, rev_angle, group, count, True)
    remaining = (float(group) - jnp.arange(group, dtype=jnp.float32))[:, None]
    rev_table = mode_powers(rate_row, rev_angle, 1.0, remaining)
    adjoint = retro + cmul(rev_table[None], later[:, None, :])
    scaled = adjoint * gain_pair
    adjoint_b = scaled.astype(jnp.bfloat16)
    boundary_adjoint = scaled[:, 0:1, :]
    out_grad = tm_scatter(
        lax.dot_general(
            states_b, misfit_b, (((0, 1), (0, 1)), ((), ())), preferred_element_type=jnp.float32
        ),
        count,
    )
    in_grad = tm_scatter(
        lax.dot_general(
            adjoint_b, signals, (((0, 1), (0, 1)), ((), ())), preferred_element_type=jnp.float32
        ),
        count,
    )
    out_square = tm_sum(jnp.sum(out_grad * out_grad), count)
    out_update = out_grad * lax.rsqrt(out_square / float(width * out_map.shape[1]) + 1e-06)
    in_square = tm_sum(jnp.sum(in_grad * in_grad), count)
    in_update = in_grad * lax.rsqrt(in_square / float(width * in_map.shape[1]) + 1e-06)
    return (out_update, in_update, boundary_adjoint)


def solution(mesh):
    return jax.shard_map(
        per_device,
        mesh=mesh,
        in_specs=(
            P("grp", "tm", None),
            P("grp", "tm", None),
            P("grp"),
            P("grp"),
            P("grp", None),
            P("grp", None),
        ),
        out_specs=(P(("grp", "tm"), None), P(("grp", "tm"), None), P("grp", "tm", None)),
        check_vma=False,
    )
```

```python
import math

import jax
import jax.numpy as jnp
from jax import lax
from jax.sharding import PartitionSpec as P


def cmul(first, second):
    half = first.shape[-1] // 2
    fr = first[..., :half]
    fi = first[..., half:]
    sr = second[..., :half]
    si = second[..., half:]
    return jnp.concatenate([fr * sr - fi * si, fr * si + fi * sr], axis=-1)


def mode_powers(decay_rate, angle, unit, counts):
    phase = jnp.mod(angle * unit, 2.0 * math.pi) * counts
    magnitude = jnp.exp(-decay_rate * unit * counts)
    return jnp.concatenate([magnitude * jnp.cos(phase), magnitude * jnp.sin(phase)], axis=-1)


def radices(count):
    sizes = []
    left = count
    while left > 1:
        size = 4 if left % 4 == 0 else (2 if left % 2 == 0 else left)
        sizes.append(size)
        left = left // size
    return sizes


def carry_in(values, rate_row, angle_row, group, count, reverse):
    unit_one = jnp.ones((1, 1), jnp.float32)

    def shifted(source, span):
        if reverse:
            pairs = [(i + span, i) for i in range(count - span)]
        else:
            pairs = [(i, i + span) for i in range(count - span)]
        return lax.ppermute(source, "tm", pairs)

    if count == 1:
        return jnp.zeros_like(values)
    sizes = radices(count)
    first = min(sizes[0], count - 1)
    acc = shifted(values, 1)
    for step in range(2, first + 1):
        factor = mode_powers(rate_row, angle_row, float(group * (step - 1)), unit_one)
        acc = acc + cmul(factor, shifted(values, step))
    span = first
    for size in sizes[1:]:
        if span >= count - 1:
            break
        moved = acc
        for step in range(1, size):
            if step * span >= count:
                break
            factor = mode_powers(rate_row, angle_row, float(group * span * step), unit_one)
            moved = moved + cmul(factor, shifted(acc, step * span))
        acc = moved
        span = span * size
    return acc


def tm_sum(value, count):
    if count & (count - 1):
        return lax.psum(value, "tm")
    span = 1
    while span < count:
        value = value + lax.ppermute(value, "tm", [(i, i ^ span) for i in range(count)])
        span = span * 2
    return value


def halving_scatter(value, count, order):
    depth = count.bit_length() - 1
    rows = value.shape[0] // count
    buf = value.reshape((2,) * depth + (rows, value.shape[1]))
    axes = list(range(depth - 1, -1, -1))
    index = lax.axis_index("tm")
    for bit in order:
        axis = axes.index(bit)
        mine = (index >> bit) & 1
        keep = lax.dynamic_index_in_dim(buf, mine, axis, keepdims=False)
        send = lax.dynamic_index_in_dim(buf, 1 - mine, axis, keepdims=False)
        buf = keep + lax.ppermute(send, "tm", [(i, i ^ (1 << bit)) for i in range(count)])
        axes.pop(axis)
    return buf.reshape(rows, value.shape[1])


def tm_scatter(value, count):
    if count & (count - 1) or count < 4:
        return lax.psum_scatter(value, "tm", scatter_dimension=0, tiled=True)
    depth = count.bit_length() - 1
    first = list(range(depth))
    second = [0, 2, 1] + list(range(3, depth))
    half = value.shape[1] // 2
    return jnp.concatenate(
        [
            halving_scatter(value[:, :half], count, first),
            halving_scatter(value[:, half:], count, second),
        ],
        axis=1,
    )


def per_device(signals, targets, decay_rate, pole_angle, in_map, out_map):
    group = signals.shape[1]
    modes = decay_rate.shape[0]
    width = 2 * modes
    count = lax.axis_size("tm")
    rate_row = decay_rate[None, :]
    fwd_angle = pole_angle[None, :]
    rev_angle = -pole_angle[None, :]
    gain = jnp.sqrt(-jnp.expm1(-2.0 * decay_rate))
    gain_pair = jnp.concatenate([gain, gain])
    unit_one = jnp.ones((1, 1), jnp.float32)
    drive = (
        lax.dot_general(
            signals, in_map, (((2,), (1,)), ((), ())), preferred_element_type=jnp.float32
        )
        * gain_pair
    )
    local = drive
    span = 1
    while span < group:
        factor = mode_powers(rate_row, fwd_angle, float(span), unit_one)
        local = jnp.concatenate(
            [local[:, :span], local[:, span:] + cmul(factor[None], local[:, :-span])], axis=1
        )
        span = span * 2
    ends = local[:, group - 1]
    entering = carry_in(ends, rate_row, fwd_angle, group, count, False)
    offsets = (jnp.arange(group, dtype=jnp.float32) + 1.0)[:, None]
    fwd_table = mode_powers(rate_row, fwd_angle, 1.0, offsets)
    states = local + cmul(fwd_table[None], entering[:, None, :])
    states_b = states.astype(jnp.bfloat16)
    predicted = lax.dot_general(
        states_b, out_map, (((2,), (0,)), ((), ())), preferred_element_type=jnp.float32
    )
    misfit_b = (predicted - targets.astype(jnp.float32)).astype(jnp.bfloat16)
    back = lax.dot_general(
        misfit_b, out_map, (((2,), (1,)), ((), ())), preferred_element_type=jnp.float32
    )
    retro = back
    span = 1
    while span < group:
        factor = mode_powers(rate_row, rev_angle, float(span), unit_one)
        retro = jnp.concatenate(
            [retro[:, :-span] + cmul(factor[None], retro[:, span:]), retro[:, group - span :]],
            axis=1,
        )
        span = span * 2
    starts = retro[:, 0]
    later = carry_in(starts, rate_row, rev_angle, group, count, True)
    remaining = (float(group) - jnp.arange(group, dtype=jnp.float32))[:, None]
    rev_table = mode_powers(rate_row, rev_angle, 1.0, remaining)
    adjoint = retro + cmul(rev_table[None], later[:, None, :])
    scaled = adjoint * gain_pair
    adjoint_b = scaled.astype(jnp.bfloat16)
    boundary_adjoint = scaled[:, 0:1, :]
    out_grad = tm_scatter(
        lax.dot_general(
            states_b, misfit_b, (((0, 1), (0, 1)), ((), ())), preferred_element_type=jnp.float32
        ),
        count,
    )
    in_grad = tm_scatter(
        lax.dot_general(
            adjoint_b, signals, (((0, 1), (0, 1)), ((), ())), preferred_element_type=jnp.float32
        ),
        count,
    )
    out_square = tm_sum(jnp.sum(out_grad * out_grad), count)
    out_update = out_grad * lax.rsqrt(out_square / float(width * out_map.shape[1]) + 1e-06)
    in_square = tm_sum(jnp.sum(in_grad * in_grad), count)
    in_update = in_grad * lax.rsqrt(in_square / float(width * in_map.shape[1]) + 1e-06)
    return (out_update, in_update, boundary_adjoint)


def solution(mesh):
    return jax.shard_map(
        per_device,
        mesh=mesh,
        in_specs=(
            P("grp", "tm", None),
            P("grp", "tm", None),
            P("grp"),
            P("grp"),
            P("grp", None),
            P("grp", None),
        ),
        out_specs=(P(("grp", "tm"), None), P(("grp", "tm"), None), P("grp", "tm", None)),
        check_vma=False,
    )
```

```python
import math

import jax
import jax.numpy as jnp
from jax import lax
from jax.sharding import PartitionSpec as P


def cmul(first, second):
    half = first.shape[-1] // 2
    fr = first[..., :half]
    fi = first[..., half:]
    sr = second[..., :half]
    si = second[..., half:]
    return jnp.concatenate([fr * sr - fi * si, fr * si + fi * sr], axis=-1)


def mode_powers(decay_rate, angle, unit, counts):
    phase = jnp.mod(angle * unit, 2.0 * math.pi) * counts
    magnitude = jnp.exp(-decay_rate * unit * counts)
    return jnp.concatenate([magnitude * jnp.cos(phase), magnitude * jnp.sin(phase)], axis=-1)


def radices(count):
    sizes = []
    left = count
    while left > 1:
        size = 4 if left % 4 == 0 else (2 if left % 2 == 0 else left)
        sizes.append(size)
        left = left // size
    return sizes


def carry_in(values, rate_row, angle_row, group, count, reverse):
    unit_one = jnp.ones((1, 1), jnp.float32)

    def shifted(source, span):
        if reverse:
            pairs = [(i + span, i) for i in range(count - span)]
        else:
            pairs = [(i, i + span) for i in range(count - span)]
        return lax.ppermute(source, "tm", pairs)

    if count == 1:
        return jnp.zeros_like(values)
    sizes = radices(count)
    first = min(sizes[0], count - 1)
    acc = shifted(values, 1)
    for step in range(2, first + 1):
        factor = mode_powers(rate_row, angle_row, float(group * (step - 1)), unit_one)
        acc = acc + cmul(factor, shifted(values, step))
    span = first
    for size in sizes[1:]:
        if span >= count - 1:
            break
        moved = acc
        for step in range(1, size):
            if step * span >= count:
                break
            factor = mode_powers(rate_row, angle_row, float(group * span * step), unit_one)
            moved = moved + cmul(factor, shifted(acc, step * span))
        acc = moved
        span = span * size
    return acc


def tm_sum(value, count):
    if count & (count - 1):
        return lax.psum(value, "tm")
    span = 1
    while span < count:
        value = value + lax.ppermute(value, "tm", [(i, i ^ span) for i in range(count)])
        span = span * 2
    return value


def halving_steps(buf, axes, order, count):
    index = lax.axis_index("tm")
    axes = list(axes)
    for bit in order:
        axis = axes.index(bit)
        mine = (index >> bit) & 1
        keep = lax.dynamic_index_in_dim(buf, mine, axis, keepdims=False)
        send = lax.dynamic_index_in_dim(buf, 1 - mine, axis, keepdims=False)
        buf = keep + lax.ppermute(send, "tm", [(i, i ^ (1 << bit)) for i in range(count)])
        axes.pop(axis)
    return buf, axes


def scatter_orders(count):
    depth = count.bit_length() - 1
    return [list(range(depth)), [0, 2, 1] + list(range(3, depth))]


def scatter_begin(value, count, lead):
    if count & (count - 1) or count < 4:
        return value
    depth = count.bit_length() - 1
    rows = value.shape[0] // count
    half = value.shape[1] // 2
    bufs = []
    for piece, order in zip((value[:, :half], value[:, half:]), scatter_orders(count)):
        buf = piece.reshape((2,) * depth + (rows, half))
        bufs.append(halving_steps(buf, range(depth - 1, -1, -1), order[:lead], count)[0])
    return bufs


def scatter_finish(bufs, count, lead):
    if count & (count - 1) or count < 4:
        return lax.psum_scatter(bufs, "tm", scatter_dimension=0, tiled=True)
    depth = count.bit_length() - 1
    parts = []
    for buf, order in zip(bufs, scatter_orders(count)):
        axes = [bit for bit in range(depth - 1, -1, -1) if bit not in order[:lead]]
        done = halving_steps(buf, axes, order[lead:], count)[0]
        parts.append(done.reshape(done.shape[-2:]))
    return jnp.concatenate(parts, axis=1)


def per_device(signals, targets, decay_rate, pole_angle, in_map, out_map):
    group = signals.shape[1]
    modes = decay_rate.shape[0]
    width = 2 * modes
    count = lax.axis_size("tm")
    rate_row = decay_rate[None, :]
    fwd_angle = pole_angle[None, :]
    rev_angle = -pole_angle[None, :]
    gain = jnp.sqrt(-jnp.expm1(-2.0 * decay_rate))
    gain_pair = jnp.concatenate([gain, gain])
    unit_one = jnp.ones((1, 1), jnp.float32)
    drive = (
        lax.dot_general(
            signals, in_map, (((2,), (1,)), ((), ())), preferred_element_type=jnp.float32
        )
        * gain_pair
    )
    local = drive
    span = 1
    while span < group:
        factor = mode_powers(rate_row, fwd_angle, float(span), unit_one)
        local = jnp.concatenate(
            [local[:, :span], local[:, span:] + cmul(factor[None], local[:, :-span])], axis=1
        )
        span = span * 2
    ends = local[:, group - 1]
    entering = carry_in(ends, rate_row, fwd_angle, group, count, False)
    offsets = (jnp.arange(group, dtype=jnp.float32) + 1.0)[:, None]
    fwd_table = mode_powers(rate_row, fwd_angle, 1.0, offsets)
    states = local + cmul(fwd_table[None], entering[:, None, :])
    states_b = states.astype(jnp.bfloat16)
    predicted = lax.dot_general(
        states_b, out_map, (((2,), (0,)), ((), ())), preferred_element_type=jnp.float32
    )
    misfit_b = (predicted - targets.astype(jnp.float32)).astype(jnp.bfloat16)
    back = lax.dot_general(
        misfit_b, out_map, (((2,), (1,)), ((), ())), preferred_element_type=jnp.float32
    )
    retro = back
    span = 1
    while span < group:
        factor = mode_powers(rate_row, rev_angle, float(span), unit_one)
        retro = jnp.concatenate(
            [retro[:, :-span] + cmul(factor[None], retro[:, span:]), retro[:, group - span :]],
            axis=1,
        )
        span = span * 2
    starts = retro[:, 0]
    later = carry_in(starts, rate_row, rev_angle, group, count, True)
    remaining = (float(group) - jnp.arange(group, dtype=jnp.float32))[:, None]
    rev_table = mode_powers(rate_row, rev_angle, 1.0, remaining)
    adjoint = retro + cmul(rev_table[None], later[:, None, :])
    scaled = adjoint * gain_pair
    adjoint_b = scaled.astype(jnp.bfloat16)
    boundary_adjoint = scaled[:, 0:1, :]
    out_bufs = scatter_begin(
        lax.dot_general(
            states_b, misfit_b, (((0, 1), (0, 1)), ((), ())), preferred_element_type=jnp.float32
        ),
        count,
        1,
    )
    adjoint_b, out_bufs = lax.optimization_barrier((adjoint_b, out_bufs))
    out_grad = scatter_finish(out_bufs, count, 1)
    in_grad = scatter_finish(
        scatter_begin(
            lax.dot_general(
                adjoint_b, signals, (((0, 1), (0, 1)), ((), ())), preferred_element_type=jnp.float32
            ),
            count,
            0,
        ),
        count,
        0,
    )
    out_square = tm_sum(jnp.sum(out_grad * out_grad), count)
    out_update = out_grad * lax.rsqrt(out_square / float(width * out_map.shape[1]) + 1e-06)
    in_square = tm_sum(jnp.sum(in_grad * in_grad), count)
    in_update = in_grad * lax.rsqrt(in_square / float(width * in_map.shape[1]) + 1e-06)
    return (out_update, in_update, boundary_adjoint)


def solution(mesh):
    return jax.shard_map(
        per_device,
        mesh=mesh,
        in_specs=(
            P("grp", "tm", None),
            P("grp", "tm", None),
            P("grp"),
            P("grp"),
            P("grp", None),
            P("grp", None),
        ),
        out_specs=(P(("grp", "tm"), None), P(("grp", "tm"), None), P("grp", "tm", None)),
        check_vma=False,
    )
```

```python
import math

import jax
import jax.numpy as jnp
from jax import lax
from jax.sharding import PartitionSpec as P


def cmul(first, second):
    half = first.shape[-1] // 2
    fr = first[..., :half]
    fi = first[..., half:]
    sr = second[..., :half]
    si = second[..., half:]
    return jnp.concatenate([fr * sr - fi * si, fr * si + fi * sr], axis=-1)


def mode_powers(decay_rate, angle, unit, counts):
    phase = jnp.mod(angle * unit, 2.0 * math.pi) * counts
    magnitude = jnp.exp(-decay_rate * unit * counts)
    return jnp.concatenate([magnitude * jnp.cos(phase), magnitude * jnp.sin(phase)], axis=-1)


def radices(count):
    sizes = []
    left = count
    while left > 1:
        size = 4 if left % 4 == 0 else (2 if left % 2 == 0 else left)
        sizes.append(size)
        left = left // size
    return sizes


def carry_in(values, rate_row, angle_row, group, count, reverse):
    unit_one = jnp.ones((1, 1), jnp.float32)

    def shifted(source, span):
        if reverse:
            pairs = [(i + span, i) for i in range(count - span)]
        else:
            pairs = [(i, i + span) for i in range(count - span)]
        return lax.ppermute(source, "tm", pairs)

    if count == 1:
        return jnp.zeros_like(values)
    sizes = radices(count)
    first = min(sizes[0], count - 1)
    acc = shifted(values, 1)
    for step in range(2, first + 1):
        factor = mode_powers(rate_row, angle_row, float(group * (step - 1)), unit_one)
        acc = acc + cmul(factor, shifted(values, step))
    span = first
    for size in sizes[1:]:
        if span >= count - 1:
            break
        moved = acc
        for step in range(1, size):
            if step * span >= count:
                break
            factor = mode_powers(rate_row, angle_row, float(group * span * step), unit_one)
            moved = moved + cmul(factor, shifted(acc, step * span))
        acc = moved
        span = span * size
    return acc


def tm_sum(value, count):
    if count & (count - 1):
        return lax.psum(value, "tm")
    span = 1
    while span < count:
        value = value + lax.ppermute(value, "tm", [(i, i ^ span) for i in range(count)])
        span = span * 2
    return value


def halving_steps(buf, axes, order, count):
    index = lax.axis_index("tm")
    axes = list(axes)
    for bit in order:
        axis = axes.index(bit)
        mine = (index >> bit) & 1
        keep = lax.dynamic_index_in_dim(buf, mine, axis, keepdims=False)
        send = lax.dynamic_index_in_dim(buf, 1 - mine, axis, keepdims=False)
        buf = keep + lax.ppermute(send, "tm", [(i, i ^ (1 << bit)) for i in range(count)])
        axes.pop(axis)
    return buf, axes


def scatter_orders(count):
    depth = count.bit_length() - 1
    return [list(range(depth)), [0, 2, 1] + list(range(3, depth))]


def scatter_begin(value, count, lead):
    if count & (count - 1) or count < 4:
        return value
    depth = count.bit_length() - 1
    rows = value.shape[0] // count
    half = value.shape[1] // 2
    bufs = []
    for piece, order in zip((value[:, :half], value[:, half:]), scatter_orders(count)):
        buf = piece.reshape((2,) * depth + (rows, half))
        bufs.append(halving_steps(buf, range(depth - 1, -1, -1), order[:lead], count)[0])
    return bufs


def scatter_finish(bufs, count, lead):
    if count & (count - 1) or count < 4:
        return lax.psum_scatter(bufs, "tm", scatter_dimension=0, tiled=True)
    depth = count.bit_length() - 1
    parts = []
    for buf, order in zip(bufs, scatter_orders(count)):
        axes = [bit for bit in range(depth - 1, -1, -1) if bit not in order[:lead]]
        done = halving_steps(buf, axes, order[lead:], count)[0]
        parts.append(done.reshape(done.shape[-2:]))
    return jnp.concatenate(parts, axis=1)


def per_device(signals, targets, decay_rate, pole_angle, in_map, out_map):
    group = signals.shape[1]
    modes = decay_rate.shape[0]
    width = 2 * modes
    count = lax.axis_size("tm")
    rate_row = decay_rate[None, :]
    fwd_angle = pole_angle[None, :]
    rev_angle = -pole_angle[None, :]
    gain = jnp.sqrt(-jnp.expm1(-2.0 * decay_rate))
    gain_pair = jnp.concatenate([gain, gain])
    unit_one = jnp.ones((1, 1), jnp.float32)
    drive = (
        lax.dot_general(
            signals, in_map, (((2,), (1,)), ((), ())), preferred_element_type=jnp.float32
        )
        * gain_pair
    )
    local = drive
    span = 1
    while span < group:
        factor = mode_powers(rate_row, fwd_angle, float(span), unit_one)
        local = jnp.concatenate(
            [local[:, :span], local[:, span:] + cmul(factor[None], local[:, :-span])], axis=1
        )
        span = span * 2
    ends = local[:, group - 1]
    entering = carry_in(ends, rate_row, fwd_angle, group, count, False)
    offsets = (jnp.arange(group, dtype=jnp.float32) + 1.0)[:, None]
    fwd_table = mode_powers(rate_row, fwd_angle, 1.0, offsets)
    states = local + cmul(fwd_table[None], entering[:, None, :])
    states_b = states.astype(jnp.bfloat16)
    predicted = lax.dot_general(
        states_b, out_map, (((2,), (0,)), ((), ())), preferred_element_type=jnp.float32
    )
    error = predicted - targets.astype(jnp.float32)
    misfit_b = error.astype(jnp.bfloat16)
    paired = not (count & (count - 1)) and count >= 4
    if paired:
        block = width // count
        core = lax.axis_index("tm") & 1
        columns = states.reshape(states.shape[0], group, width // (2 * block), 2, block)
        own_cols = lax.dynamic_index_in_dim(columns, core, 3, keepdims=False)
        other_cols = lax.dynamic_index_in_dim(columns, 1 - core, 3, keepdims=False)
        partner = [(i, i ^ 1) for i in range(count)]
        zero = decay_rate[0] * 0.0
        got_cols = (lax.ppermute(other_cols, "tm", partner) + zero).astype(jnp.bfloat16)
        got_error = (lax.ppermute(error, "tm", partner) + zero).astype(jnp.bfloat16)
        both_states = jnp.concatenate([own_cols.astype(jnp.bfloat16), got_cols], axis=1)
        both_misfit = jnp.concatenate([misfit_b, got_error], axis=1)
        out_half = lax.dot_general(
            both_states.reshape(states.shape[0], 2 * group, width // 2),
            both_misfit,
            (((0, 1), (0, 1)), ((), ())),
            preferred_element_type=jnp.float32,
        )
    back = lax.dot_general(
        misfit_b, out_map, (((2,), (1,)), ((), ())), preferred_element_type=jnp.float32
    )
    retro = back
    span = 1
    while span < group:
        factor = mode_powers(rate_row, rev_angle, float(span), unit_one)
        retro = jnp.concatenate(
            [retro[:, :-span] + cmul(factor[None], retro[:, span:]), retro[:, group - span :]],
            axis=1,
        )
        span = span * 2
    starts = retro[:, 0]
    later = carry_in(starts, rate_row, rev_angle, group, count, True)
    remaining = (float(group) - jnp.arange(group, dtype=jnp.float32))[:, None]
    rev_table = mode_powers(rate_row, rev_angle, 1.0, remaining)
    adjoint = retro + cmul(rev_table[None], later[:, None, :])
    scaled = adjoint * gain_pair
    adjoint_b = scaled.astype(jnp.bfloat16)
    boundary_adjoint = scaled[:, 0:1, :]
    if paired:
        depth = count.bit_length() - 1
        split = out_half.shape[1] // 2
        out_bufs = [
            piece.reshape((2,) * (depth - 1) + (block, split))
            for piece in (out_half[:, :split], out_half[:, split:])
        ]
        adjoint_b, out_bufs = lax.optimization_barrier((adjoint_b, out_bufs))
        out_grad = scatter_finish(out_bufs, count, 1)
    else:
        out_grad = lax.psum_scatter(
            lax.dot_general(
                states_b, misfit_b, (((0, 1), (0, 1)), ((), ())), preferred_element_type=jnp.float32
            ),
            "tm",
            scatter_dimension=0,
            tiled=True,
        )
    in_grad = scatter_finish(
        scatter_begin(
            lax.dot_general(
                adjoint_b, signals, (((0, 1), (0, 1)), ((), ())), preferred_element_type=jnp.float32
            ),
            count,
            0,
        ),
        count,
        0,
    )
    out_square = tm_sum(jnp.sum(out_grad * out_grad), count)
    out_update = out_grad * lax.rsqrt(out_square / float(width * out_map.shape[1]) + 1e-06)
    in_square = tm_sum(jnp.sum(in_grad * in_grad), count)
    in_update = in_grad * lax.rsqrt(in_square / float(width * in_map.shape[1]) + 1e-06)
    return (out_update, in_update, boundary_adjoint)


def solution(mesh):
    return jax.shard_map(
        per_device,
        mesh=mesh,
        in_specs=(
            P("grp", "tm", None),
            P("grp", "tm", None),
            P("grp"),
            P("grp"),
            P("grp", None),
            P("grp", None),
        ),
        out_specs=(P(("grp", "tm"), None), P(("grp", "tm"), None), P("grp", "tm", None)),
        check_vma=False,
    )
```

```python
import math

import jax
import jax.numpy as jnp
from jax import lax
from jax.sharding import PartitionSpec as P


def cmul(first, second):
    half = first.shape[-1] // 2
    fr = first[..., :half]
    fi = first[..., half:]
    sr = second[..., :half]
    si = second[..., half:]
    return jnp.concatenate([fr * sr - fi * si, fr * si + fi * sr], axis=-1)


def mode_powers(decay_rate, angle, unit, counts):
    phase = jnp.mod(angle * unit, 2.0 * math.pi) * counts
    magnitude = jnp.exp(-decay_rate * unit * counts)
    return jnp.concatenate([magnitude * jnp.cos(phase), magnitude * jnp.sin(phase)], axis=-1)


def radices(count):
    sizes = []
    left = count
    while left > 1:
        size = 4 if left % 4 == 0 else (2 if left % 2 == 0 else left)
        sizes.append(size)
        left = left // size
    return sizes


def carry_in(values, rate_row, angle_row, group, count, reverse):
    unit_one = jnp.ones((1, 1), jnp.float32)

    def shifted(source, span):
        if reverse:
            pairs = [(i + span, i) for i in range(count - span)]
        else:
            pairs = [(i, i + span) for i in range(count - span)]
        return lax.ppermute(source, "tm", pairs)

    if count == 1:
        return jnp.zeros_like(values)
    sizes = radices(count)
    first = min(sizes[0], count - 1)
    acc = shifted(values, 1)
    for step in range(2, first + 1):
        factor = mode_powers(rate_row, angle_row, float(group * (step - 1)), unit_one)
        acc = acc + cmul(factor, shifted(values, step))
    span = first
    for size in sizes[1:]:
        if span >= count - 1:
            break
        moved = acc
        for step in range(1, size):
            if step * span >= count:
                break
            factor = mode_powers(rate_row, angle_row, float(group * span * step), unit_one)
            moved = moved + cmul(factor, shifted(acc, step * span))
        acc = moved
        span = span * size
    return acc


def tm_sum(value, count):
    if count & (count - 1):
        return lax.psum(value, "tm")
    span = 1
    while span < count:
        value = value + lax.ppermute(value, "tm", [(i, i ^ span) for i in range(count)])
        span = span * 2
    return value


def halving_steps(buf, axes, order, count):
    index = lax.axis_index("tm")
    axes = list(axes)
    for bit in order:
        axis = axes.index(bit)
        mine = (index >> bit) & 1
        keep = lax.dynamic_index_in_dim(buf, mine, axis, keepdims=False)
        send = lax.dynamic_index_in_dim(buf, 1 - mine, axis, keepdims=False)
        buf = keep + lax.ppermute(send, "tm", [(i, i ^ (1 << bit)) for i in range(count)])
        axes.pop(axis)
    return buf, axes


def scatter_orders(count):
    depth = count.bit_length() - 1
    return [list(range(depth)), [0, 2, 3, 1] + list(range(4, depth))]


def scatter_begin(value, count, lead):
    if count & (count - 1) or count < 4:
        return value
    depth = count.bit_length() - 1
    rows = value.shape[0] // count
    half = value.shape[1] // 2
    bufs = []
    for piece, order in zip((value[:, :half], value[:, half:]), scatter_orders(count)):
        buf = piece.reshape((2,) * depth + (rows, half))
        bufs.append(halving_steps(buf, range(depth - 1, -1, -1), order[:lead], count)[0])
    return bufs


def scatter_finish(bufs, count, lead):
    if count & (count - 1) or count < 4:
        return lax.psum_scatter(bufs, "tm", scatter_dimension=0, tiled=True)
    depth = count.bit_length() - 1
    parts = []
    for buf, order in zip(bufs, scatter_orders(count)):
        axes = [bit for bit in range(depth - 1, -1, -1) if bit not in order[:lead]]
        done = halving_steps(buf, axes, order[lead:], count)[0]
        parts.append(done.reshape(done.shape[-2:]))
    return jnp.concatenate(parts, axis=1)


def per_device(signals, targets, decay_rate, pole_angle, in_map, out_map):
    group = signals.shape[1]
    modes = decay_rate.shape[0]
    width = 2 * modes
    count = lax.axis_size("tm")
    rate_row = decay_rate[None, :]
    fwd_angle = pole_angle[None, :]
    rev_angle = -pole_angle[None, :]
    gain = jnp.sqrt(-jnp.expm1(-2.0 * decay_rate))
    gain_pair = jnp.concatenate([gain, gain])
    unit_one = jnp.ones((1, 1), jnp.float32)
    drive = (
        lax.dot_general(
            signals, in_map, (((2,), (1,)), ((), ())), preferred_element_type=jnp.float32
        )
        * gain_pair
    )
    local = drive
    span = 1
    while span < group:
        factor = mode_powers(rate_row, fwd_angle, float(span), unit_one)
        local = jnp.concatenate(
            [local[:, :span], local[:, span:] + cmul(factor[None], local[:, :-span])], axis=1
        )
        span = span * 2
    ends = local[:, group - 1]
    entering = carry_in(ends, rate_row, fwd_angle, group, count, False)
    offsets = (jnp.arange(group, dtype=jnp.float32) + 1.0)[:, None]
    fwd_table = mode_powers(rate_row, fwd_angle, 1.0, offsets)
    states = local + cmul(fwd_table[None], entering[:, None, :])
    states_b = states.astype(jnp.bfloat16)
    predicted = lax.dot_general(
        states_b, out_map, (((2,), (0,)), ((), ())), preferred_element_type=jnp.float32
    )
    misfit_b = (predicted - targets.astype(jnp.float32)).astype(jnp.bfloat16)
    back = lax.dot_general(
        misfit_b, out_map, (((2,), (1,)), ((), ())), preferred_element_type=jnp.float32
    )
    retro = back
    span = 1
    while span < group:
        factor = mode_powers(rate_row, rev_angle, float(span), unit_one)
        retro = jnp.concatenate(
            [retro[:, :-span] + cmul(factor[None], retro[:, span:]), retro[:, group - span :]],
            axis=1,
        )
        span = span * 2
    starts = retro[:, 0]
    later = carry_in(starts, rate_row, rev_angle, group, count, True)
    remaining = (float(group) - jnp.arange(group, dtype=jnp.float32))[:, None]
    rev_table = mode_powers(rate_row, rev_angle, 1.0, remaining)
    adjoint = retro + cmul(rev_table[None], later[:, None, :])
    scaled = adjoint * gain_pair
    adjoint_b = scaled.astype(jnp.bfloat16)
    boundary_adjoint = scaled[:, 0:1, :]
    out_bufs = scatter_begin(
        lax.dot_general(
            states_b, misfit_b, (((0, 1), (0, 1)), ((), ())), preferred_element_type=jnp.float32
        ),
        count,
        1,
    )
    adjoint_b, out_bufs = lax.optimization_barrier((adjoint_b, out_bufs))
    out_grad = scatter_finish(out_bufs, count, 1)
    in_grad = scatter_finish(
        scatter_begin(
            lax.dot_general(
                adjoint_b, signals, (((0, 1), (0, 1)), ((), ())), preferred_element_type=jnp.float32
            ),
            count,
            0,
        ),
        count,
        0,
    )
    out_square = tm_sum(jnp.sum(out_grad * out_grad), count)
    out_update = out_grad * lax.rsqrt(out_square / float(width * out_map.shape[1]) + 1e-06)
    in_square = tm_sum(jnp.sum(in_grad * in_grad), count)
    in_update = in_grad * lax.rsqrt(in_square / float(width * in_map.shape[1]) + 1e-06)
    return (out_update, in_update, boundary_adjoint)


def solution(mesh):
    return jax.shard_map(
        per_device,
        mesh=mesh,
        in_specs=(
            P("grp", "tm", None),
            P("grp", "tm", None),
            P("grp"),
            P("grp"),
            P("grp", None),
            P("grp", None),
        ),
        out_specs=(P(("grp", "tm"), None), P(("grp", "tm"), None), P("grp", "tm", None)),
        check_vma=False,
    )
```

```python
import math

import jax
import jax.numpy as jnp
from jax import lax
from jax.sharding import PartitionSpec as P


def cmul(first, second):
    half = first.shape[-1] // 2
    fr = first[..., :half]
    fi = first[..., half:]
    sr = second[..., :half]
    si = second[..., half:]
    return jnp.concatenate([fr * sr - fi * si, fr * si + fi * sr], axis=-1)


def mode_powers(decay_rate, angle, unit, counts):
    phase = jnp.mod(angle * unit, 2.0 * math.pi) * counts
    magnitude = jnp.exp(-decay_rate * unit * counts)
    return jnp.concatenate([magnitude * jnp.cos(phase), magnitude * jnp.sin(phase)], axis=-1)


def radices(count):
    sizes = []
    left = count
    while left > 1:
        size = 4 if left % 4 == 0 else (2 if left % 2 == 0 else left)
        sizes.append(size)
        left = left // size
    return sizes


def carry_in(values, rate_row, angle_row, group, count, reverse):
    unit_one = jnp.ones((1, 1), jnp.float32)

    def shifted(source, span):
        if reverse:
            pairs = [(i + span, i) for i in range(count - span)]
        else:
            pairs = [(i, i + span) for i in range(count - span)]
        return lax.ppermute(source, "tm", pairs)

    if count == 1:
        return jnp.zeros_like(values)
    sizes = radices(count)
    first = min(sizes[0], count - 1)
    acc = shifted(values, 1)
    for step in range(2, first + 1):
        factor = mode_powers(rate_row, angle_row, float(group * (step - 1)), unit_one)
        acc = acc + cmul(factor, shifted(values, step))
    span = first
    for size in sizes[1:]:
        if span >= count - 1:
            break
        moved = acc
        for step in range(1, size):
            if step * span >= count:
                break
            factor = mode_powers(rate_row, angle_row, float(group * span * step), unit_one)
            moved = moved + cmul(factor, shifted(acc, step * span))
        acc = moved
        span = span * size
    return acc


def tm_sum(value, count):
    if count & (count - 1):
        return lax.psum(value, "tm")
    span = 1
    while span < count:
        value = value + lax.ppermute(value, "tm", [(i, i ^ span) for i in range(count)])
        span = span * 2
    return value


def halving_steps(buf, axes, order, count):
    index = lax.axis_index("tm")
    axes = list(axes)
    for bit in order:
        axis = axes.index(bit)
        mine = (index >> bit) & 1
        keep = lax.dynamic_index_in_dim(buf, mine, axis, keepdims=False)
        send = lax.dynamic_index_in_dim(buf, 1 - mine, axis, keepdims=False)
        buf = keep + lax.ppermute(send, "tm", [(i, i ^ (1 << bit)) for i in range(count)])
        axes.pop(axis)
    return buf, axes


def scatter_orders(count):
    depth = count.bit_length() - 1
    return [list(range(depth)), [0, 2, 1] + list(range(3, depth))]


def scatter_finish(bufs, count, lead):
    if count & (count - 1) or count < 4:
        return lax.psum_scatter(bufs, "tm", scatter_dimension=0, tiled=True)
    depth = count.bit_length() - 1
    parts = []
    for buf, order in zip(bufs, scatter_orders(count)):
        axes = [bit for bit in range(depth - 1, -1, -1) if bit not in order[:lead]]
        done = halving_steps(buf, axes, order[lead:], count)[0]
        parts.append(done.reshape(done.shape[-2:]))
    return jnp.concatenate(parts, axis=1)


def split_first(left, right, count):
    depth = count.bit_length() - 1
    members, steps, width = left.shape
    block = width // count
    core = lax.axis_index("tm") & 1
    cols = left.reshape(members, steps, width // (2 * block), 2, block)
    own = lax.dynamic_index_in_dim(cols, core, 3, keepdims=False).reshape(members, steps, width // 2)
    other = lax.dynamic_index_in_dim(cols, 1 - core, 3, keepdims=False).reshape(
        members, steps, width // 2
    )
    half = right.shape[2] // 2
    partner = [(i, i ^ 1) for i in range(count)]
    dims = (((0, 1), (0, 1)), ((), ()))
    bufs = []
    for piece in (right[:, :, :half], right[:, :, half:]):
        keep = lax.dot_general(own, piece, dims, preferred_element_type=jnp.float32)
        send = lax.dot_general(other, piece, dims, preferred_element_type=jnp.float32)
        buf = keep + lax.ppermute(send, "tm", partner)
        bufs.append(buf.reshape((2,) * (depth - 1) + (block, half)))
    return bufs


def per_device(signals, targets, decay_rate, pole_angle, in_map, out_map):
    group = signals.shape[1]
    modes = decay_rate.shape[0]
    width = 2 * modes
    count = lax.axis_size("tm")
    rate_row = decay_rate[None, :]
    fwd_angle = pole_angle[None, :]
    rev_angle = -pole_angle[None, :]
    gain = jnp.sqrt(-jnp.expm1(-2.0 * decay_rate))
    gain_pair = jnp.concatenate([gain, gain])
    unit_one = jnp.ones((1, 1), jnp.float32)
    drive = (
        lax.dot_general(
            signals, in_map, (((2,), (1,)), ((), ())), preferred_element_type=jnp.float32
        )
        * gain_pair
    )
    local = drive
    span = 1
    while span < group:
        factor = mode_powers(rate_row, fwd_angle, float(span), unit_one)
        local = jnp.concatenate(
            [local[:, :span], local[:, span:] + cmul(factor[None], local[:, :-span])], axis=1
        )
        span = span * 2
    ends = local[:, group - 1]
    entering = carry_in(ends, rate_row, fwd_angle, group, count, False)
    offsets = (jnp.arange(group, dtype=jnp.float32) + 1.0)[:, None]
    fwd_table = mode_powers(rate_row, fwd_angle, 1.0, offsets)
    states = local + cmul(fwd_table[None], entering[:, None, :])
    states_b = states.astype(jnp.bfloat16)
    predicted = lax.dot_general(
        states_b, out_map, (((2,), (0,)), ((), ())), preferred_element_type=jnp.float32
    )
    misfit_b = (predicted - targets.astype(jnp.float32)).astype(jnp.bfloat16)
    back = lax.dot_general(
        misfit_b, out_map, (((2,), (1,)), ((), ())), preferred_element_type=jnp.float32
    )
    retro = back
    span = 1
    while span < group:
        factor = mode_powers(rate_row, rev_angle, float(span), unit_one)
        retro = jnp.concatenate(
            [retro[:, :-span] + cmul(factor[None], retro[:, span:]), retro[:, group - span :]],
            axis=1,
        )
        span = span * 2
    starts = retro[:, 0]
    later = carry_in(starts, rate_row, rev_angle, group, count, True)
    remaining = (float(group) - jnp.arange(group, dtype=jnp.float32))[:, None]
    rev_table = mode_powers(rate_row, rev_angle, 1.0, remaining)
    adjoint = retro + cmul(rev_table[None], later[:, None, :])
    scaled = adjoint * gain_pair
    adjoint_b = scaled.astype(jnp.bfloat16)
    boundary_adjoint = scaled[:, 0:1, :]
    paired = not (count & (count - 1)) and count >= 4
    if paired:
        out_bufs = split_first(states_b, misfit_b, count)
        adjoint_b, out_bufs = lax.optimization_barrier((adjoint_b, out_bufs))
        out_grad = scatter_finish(out_bufs, count, 1)
        in_grad = scatter_finish(split_first(adjoint_b, signals, count), count, 1)
    else:
        dims = (((0, 1), (0, 1)), ((), ()))
        out_grad = lax.psum_scatter(
            lax.dot_general(states_b, misfit_b, dims, preferred_element_type=jnp.float32),
            "tm",
            scatter_dimension=0,
            tiled=True,
        )
        in_grad = lax.psum_scatter(
            lax.dot_general(adjoint_b, signals, dims, preferred_element_type=jnp.float32),
            "tm",
            scatter_dimension=0,
            tiled=True,
        )
    out_square = tm_sum(jnp.sum(out_grad * out_grad), count)
    out_update = out_grad * lax.rsqrt(out_square / float(width * out_map.shape[1]) + 1e-06)
    in_square = tm_sum(jnp.sum(in_grad * in_grad), count)
    in_update = in_grad * lax.rsqrt(in_square / float(width * in_map.shape[1]) + 1e-06)
    return (out_update, in_update, boundary_adjoint)


def solution(mesh):
    return jax.shard_map(
        per_device,
        mesh=mesh,
        in_specs=(
            P("grp", "tm", None),
            P("grp", "tm", None),
            P("grp"),
            P("grp"),
            P("grp", None),
            P("grp", None),
        ),
        out_specs=(P(("grp", "tm"), None), P(("grp", "tm"), None), P("grp", "tm", None)),
        check_vma=False,
    )
```

```python
import math

import jax
import jax.numpy as jnp
from jax import lax
from jax.sharding import PartitionSpec as P


def cmul(first, second):
    half = first.shape[-1] // 2
    fr = first[..., :half]
    fi = first[..., half:]
    sr = second[..., :half]
    si = second[..., half:]
    return jnp.concatenate([fr * sr - fi * si, fr * si + fi * sr], axis=-1)


def mode_powers(decay_rate, angle, unit, counts):
    phase = jnp.mod(angle * unit, 2.0 * math.pi) * counts
    magnitude = jnp.exp(-decay_rate * unit * counts)
    return jnp.concatenate([magnitude * jnp.cos(phase), magnitude * jnp.sin(phase)], axis=-1)


def radices(count):
    sizes = []
    left = count
    while left > 1:
        size = 4 if left % 4 == 0 else (2 if left % 2 == 0 else left)
        sizes.append(size)
        left = left // size
    return sizes


def carry_in(values, rate_row, angle_row, group, count, reverse):
    unit_one = jnp.ones((1, 1), jnp.float32)

    def shifted(source, span):
        if reverse:
            pairs = [(i + span, i) for i in range(count - span)]
        else:
            pairs = [(i, i + span) for i in range(count - span)]
        return lax.ppermute(source, "tm", pairs)

    if count == 1:
        return jnp.zeros_like(values)
    sizes = radices(count)
    first = min(sizes[0], count - 1)
    acc = shifted(values, 1)
    for step in range(2, first + 1):
        factor = mode_powers(rate_row, angle_row, float(group * (step - 1)), unit_one)
        acc = acc + cmul(factor, shifted(values, step))
    span = first
    for size in sizes[1:]:
        if span >= count - 1:
            break
        moved = acc
        for step in range(1, size):
            if step * span >= count:
                break
            factor = mode_powers(rate_row, angle_row, float(group * span * step), unit_one)
            moved = moved + cmul(factor, shifted(acc, step * span))
        acc = moved
        span = span * size
    return acc


def tm_sum(value, count):
    if count & (count - 1):
        return lax.psum(value, "tm")
    span = 1
    while span < count:
        value = value + lax.ppermute(value, "tm", [(i, i ^ span) for i in range(count)])
        span = span * 2
    return value


def halving_steps(buf, axes, order, count):
    index = lax.axis_index("tm")
    axes = list(axes)
    for bit in order:
        axis = axes.index(bit)
        mine = (index >> bit) & 1
        keep = lax.dynamic_index_in_dim(buf, mine, axis, keepdims=False)
        send = lax.dynamic_index_in_dim(buf, 1 - mine, axis, keepdims=False)
        buf = keep + lax.ppermute(send, "tm", [(i, i ^ (1 << bit)) for i in range(count)])
        axes.pop(axis)
    return buf, axes


def scatter_orders(count):
    depth = count.bit_length() - 1
    return [list(range(depth)), [0, 2, 1] + list(range(3, depth))]


def scatter_begin(pieces, count, lead):
    depth = count.bit_length() - 1
    rows = pieces[0].shape[0] // count
    bufs = []
    for piece, order in zip(pieces, scatter_orders(count)):
        buf = piece.reshape((2,) * depth + (rows, piece.shape[1]))
        bufs.append(halving_steps(buf, range(depth - 1, -1, -1), order[:lead], count)[0])
    return bufs


def column_halves(left, right):
    half = right.shape[2] // 2
    dims = (((0, 1), (0, 1)), ((), ()))
    return [
        lax.dot_general(left, piece, dims, preferred_element_type=jnp.float32)
        for piece in (right[:, :, :half], right[:, :, half:])
    ]


def scatter_finish(bufs, count, lead):
    if count & (count - 1) or count < 4:
        return lax.psum_scatter(bufs, "tm", scatter_dimension=0, tiled=True)
    depth = count.bit_length() - 1
    parts = []
    for buf, order in zip(bufs, scatter_orders(count)):
        axes = [bit for bit in range(depth - 1, -1, -1) if bit not in order[:lead]]
        done = halving_steps(buf, axes, order[lead:], count)[0]
        parts.append(done.reshape(done.shape[-2:]))
    return jnp.concatenate(parts, axis=1)


def per_device(signals, targets, decay_rate, pole_angle, in_map, out_map):
    group = signals.shape[1]
    modes = decay_rate.shape[0]
    width = 2 * modes
    count = lax.axis_size("tm")
    rate_row = decay_rate[None, :]
    fwd_angle = pole_angle[None, :]
    rev_angle = -pole_angle[None, :]
    gain = jnp.sqrt(-jnp.expm1(-2.0 * decay_rate))
    gain_pair = jnp.concatenate([gain, gain])
    unit_one = jnp.ones((1, 1), jnp.float32)
    drive = (
        lax.dot_general(
            signals, in_map, (((2,), (1,)), ((), ())), preferred_element_type=jnp.float32
        )
        * gain_pair
    )
    local = drive
    span = 1
    while span < group:
        factor = mode_powers(rate_row, fwd_angle, float(span), unit_one)
        local = jnp.concatenate(
            [local[:, :span], local[:, span:] + cmul(factor[None], local[:, :-span])], axis=1
        )
        span = span * 2
    ends = local[:, group - 1]
    entering = carry_in(ends, rate_row, fwd_angle, group, count, False)
    offsets = (jnp.arange(group, dtype=jnp.float32) + 1.0)[:, None]
    fwd_table = mode_powers(rate_row, fwd_angle, 1.0, offsets)
    states = local + cmul(fwd_table[None], entering[:, None, :])
    states_b = states.astype(jnp.bfloat16)
    predicted = lax.dot_general(
        states_b, out_map, (((2,), (0,)), ((), ())), preferred_element_type=jnp.float32
    )
    misfit_b = (predicted - targets.astype(jnp.float32)).astype(jnp.bfloat16)
    back = lax.dot_general(
        misfit_b, out_map, (((2,), (1,)), ((), ())), preferred_element_type=jnp.float32
    )
    retro = back
    span = 1
    while span < group:
        factor = mode_powers(rate_row, rev_angle, float(span), unit_one)
        retro = jnp.concatenate(
            [retro[:, :-span] + cmul(factor[None], retro[:, span:]), retro[:, group - span :]],
            axis=1,
        )
        span = span * 2
    starts = retro[:, 0]
    later = carry_in(starts, rate_row, rev_angle, group, count, True)
    remaining = (float(group) - jnp.arange(group, dtype=jnp.float32))[:, None]
    rev_table = mode_powers(rate_row, rev_angle, 1.0, remaining)
    adjoint = retro + cmul(rev_table[None], later[:, None, :])
    scaled = adjoint * gain_pair
    adjoint_b = scaled.astype(jnp.bfloat16)
    boundary_adjoint = scaled[:, 0:1, :]
    if not (count & (count - 1)) and count >= 4:
        out_bufs = scatter_begin(column_halves(states_b, misfit_b), count, 1)
        adjoint_b, out_bufs = lax.optimization_barrier((adjoint_b, out_bufs))
        out_grad = scatter_finish(out_bufs, count, 1)
        in_grad = scatter_finish(
            scatter_begin(column_halves(adjoint_b, signals), count, 0), count, 0
        )
    else:
        out_grad = jnp.concatenate(
            [
                lax.psum_scatter(part, "tm", scatter_dimension=0, tiled=True)
                for part in column_halves(states_b, misfit_b)
            ],
            axis=1,
        )
        in_grad = jnp.concatenate(
            [
                lax.psum_scatter(part, "tm", scatter_dimension=0, tiled=True)
                for part in column_halves(adjoint_b, signals)
            ],
            axis=1,
        )
    out_square = tm_sum(jnp.sum(out_grad * out_grad), count)
    out_update = out_grad * lax.rsqrt(out_square / float(width * out_map.shape[1]) + 1e-06)
    in_square = tm_sum(jnp.sum(in_grad * in_grad), count)
    in_update = in_grad * lax.rsqrt(in_square / float(width * in_map.shape[1]) + 1e-06)
    return (out_update, in_update, boundary_adjoint)


def solution(mesh):
    return jax.shard_map(
        per_device,
        mesh=mesh,
        in_specs=(
            P("grp", "tm", None),
            P("grp", "tm", None),
            P("grp"),
            P("grp"),
            P("grp", None),
            P("grp", None),
        ),
        out_specs=(P(("grp", "tm"), None), P(("grp", "tm"), None), P("grp", "tm", None)),
        check_vma=False,
    )
```

```python
import math

import jax
import jax.numpy as jnp
from jax import lax
from jax.sharding import PartitionSpec as P


PIECES = 4


def cmul(first, second):
    half = first.shape[-1] // 2
    fr = first[..., :half]
    fi = first[..., half:]
    sr = second[..., :half]
    si = second[..., half:]
    return jnp.concatenate([fr * sr - fi * si, fr * si + fi * sr], axis=-1)


def mode_powers(decay_rate, angle, unit, counts):
    phase = jnp.mod(angle * unit, 2.0 * math.pi) * counts
    magnitude = jnp.exp(-decay_rate * unit * counts)
    return jnp.concatenate([magnitude * jnp.cos(phase), magnitude * jnp.sin(phase)], axis=-1)


def radices(count):
    sizes = []
    left = count
    while left > 1:
        size = 4 if left % 4 == 0 else (2 if left % 2 == 0 else left)
        sizes.append(size)
        left = left // size
    return sizes


def carry_in(values, rate_row, angle_row, group, count, reverse):
    unit_one = jnp.ones((1, 1), jnp.float32)

    def shifted(source, span):
        if reverse:
            pairs = [(i + span, i) for i in range(count - span)]
        else:
            pairs = [(i, i + span) for i in range(count - span)]
        return lax.ppermute(source, "tm", pairs)

    if count == 1:
        return jnp.zeros_like(values)
    sizes = radices(count)
    first = min(sizes[0], count - 1)
    acc = shifted(values, 1)
    for step in range(2, first + 1):
        factor = mode_powers(rate_row, angle_row, float(group * (step - 1)), unit_one)
        acc = acc + cmul(factor, shifted(values, step))
    span = first
    for size in sizes[1:]:
        if span >= count - 1:
            break
        moved = acc
        for step in range(1, size):
            if step * span >= count:
                break
            factor = mode_powers(rate_row, angle_row, float(group * span * step), unit_one)
            moved = moved + cmul(factor, shifted(acc, step * span))
        acc = moved
        span = span * size
    return acc


def tm_sum(value, count):
    if count & (count - 1):
        return lax.psum(value, "tm")
    span = 1
    while span < count:
        value = value + lax.ppermute(value, "tm", [(i, i ^ span) for i in range(count)])
        span = span * 2
    return value


def halving_steps(buf, axes, order, count):
    index = lax.axis_index("tm")
    axes = list(axes)
    for bit in order:
        axis = axes.index(bit)
        mine = (index >> bit) & 1
        keep = lax.dynamic_index_in_dim(buf, mine, axis, keepdims=False)
        send = lax.dynamic_index_in_dim(buf, 1 - mine, axis, keepdims=False)
        buf = keep + lax.ppermute(send, "tm", [(i, i ^ (1 << bit)) for i in range(count)])
        axes.pop(axis)
    return buf, axes


def scatter_orders(count):
    depth = count.bit_length() - 1
    first = list(range(depth))
    second = [0, 2, 1] + list(range(3, depth))
    return [first, second] * (PIECES // 2)


def scatter_begin(pieces, count, lead):
    depth = count.bit_length() - 1
    rows = pieces[0].shape[0] // count
    bufs = []
    for piece, order in zip(pieces, scatter_orders(count)):
        buf = piece.reshape((2,) * depth + (rows, piece.shape[1]))
        bufs.append(halving_steps(buf, range(depth - 1, -1, -1), order[:lead], count)[0])
    return bufs


def column_halves(left, right):
    width = right.shape[2] // PIECES
    dims = (((0, 1), (0, 1)), ((), ()))
    return [
        lax.dot_general(
            left, right[:, :, k * width : (k + 1) * width], dims, preferred_element_type=jnp.float32
        )
        for k in range(PIECES)
    ]


def scatter_finish(bufs, count, lead):
    if count & (count - 1) or count < 4:
        return lax.psum_scatter(bufs, "tm", scatter_dimension=0, tiled=True)
    depth = count.bit_length() - 1
    parts = []
    for buf, order in zip(bufs, scatter_orders(count)):
        axes = [bit for bit in range(depth - 1, -1, -1) if bit not in order[:lead]]
        done = halving_steps(buf, axes, order[lead:], count)[0]
        parts.append(done.reshape(done.shape[-2:]))
    return jnp.concatenate(parts, axis=1)


def per_device(signals, targets, decay_rate, pole_angle, in_map, out_map):
    group = signals.shape[1]
    modes = decay_rate.shape[0]
    width = 2 * modes
    count = lax.axis_size("tm")
    rate_row = decay_rate[None, :]
    fwd_angle = pole_angle[None, :]
    rev_angle = -pole_angle[None, :]
    gain = jnp.sqrt(-jnp.expm1(-2.0 * decay_rate))
    gain_pair = jnp.concatenate([gain, gain])
    unit_one = jnp.ones((1, 1), jnp.float32)
    drive = (
        lax.dot_general(
            signals, in_map, (((2,), (1,)), ((), ())), preferred_element_type=jnp.float32
        )
        * gain_pair
    )
    local = drive
    span = 1
    while span < group:
        factor = mode_powers(rate_row, fwd_angle, float(span), unit_one)
        local = jnp.concatenate(
            [local[:, :span], local[:, span:] + cmul(factor[None], local[:, :-span])], axis=1
        )
        span = span * 2
    ends = local[:, group - 1]
    entering = carry_in(ends, rate_row, fwd_angle, group, count, False)
    offsets = (jnp.arange(group, dtype=jnp.float32) + 1.0)[:, None]
    fwd_table = mode_powers(rate_row, fwd_angle, 1.0, offsets)
    states = local + cmul(fwd_table[None], entering[:, None, :])
    states_b = states.astype(jnp.bfloat16)
    predicted = lax.dot_general(
        states_b, out_map, (((2,), (0,)), ((), ())), preferred_element_type=jnp.float32
    )
    misfit_b = (predicted - targets.astype(jnp.float32)).astype(jnp.bfloat16)
    back = lax.dot_general(
        misfit_b, out_map, (((2,), (1,)), ((), ())), preferred_element_type=jnp.float32
    )
    retro = back
    span = 1
    while span < group:
        factor = mode_powers(rate_row, rev_angle, float(span), unit_one)
        retro = jnp.concatenate(
            [retro[:, :-span] + cmul(factor[None], retro[:, span:]), retro[:, group - span :]],
            axis=1,
        )
        span = span * 2
    starts = retro[:, 0]
    later = carry_in(starts, rate_row, rev_angle, group, count, True)
    remaining = (float(group) - jnp.arange(group, dtype=jnp.float32))[:, None]
    rev_table = mode_powers(rate_row, rev_angle, 1.0, remaining)
    adjoint = retro + cmul(rev_table[None], later[:, None, :])
    scaled = adjoint * gain_pair
    adjoint_b = scaled.astype(jnp.bfloat16)
    boundary_adjoint = scaled[:, 0:1, :]
    if not (count & (count - 1)) and count >= 4:
        out_bufs = scatter_begin(column_halves(states_b, misfit_b), count, 1)
        adjoint_b, out_bufs = lax.optimization_barrier((adjoint_b, out_bufs))
        out_grad = scatter_finish(out_bufs, count, 1)
        in_grad = scatter_finish(
            scatter_begin(column_halves(adjoint_b, signals), count, 0), count, 0
        )
    else:
        out_grad = jnp.concatenate(
            [
                lax.psum_scatter(part, "tm", scatter_dimension=0, tiled=True)
                for part in column_halves(states_b, misfit_b)
            ],
            axis=1,
        )
        in_grad = jnp.concatenate(
            [
                lax.psum_scatter(part, "tm", scatter_dimension=0, tiled=True)
                for part in column_halves(adjoint_b, signals)
            ],
            axis=1,
        )
    out_square = tm_sum(jnp.sum(out_grad * out_grad), count)
    out_update = out_grad * lax.rsqrt(out_square / float(width * out_map.shape[1]) + 1e-06)
    in_square = tm_sum(jnp.sum(in_grad * in_grad), count)
    in_update = in_grad * lax.rsqrt(in_square / float(width * in_map.shape[1]) + 1e-06)
    return (out_update, in_update, boundary_adjoint)


def solution(mesh):
    return jax.shard_map(
        per_device,
        mesh=mesh,
        in_specs=(
            P("grp", "tm", None),
            P("grp", "tm", None),
            P("grp"),
            P("grp"),
            P("grp", None),
            P("grp", None),
        ),
        out_specs=(P(("grp", "tm"), None), P(("grp", "tm"), None), P("grp", "tm", None)),
        check_vma=False,
    )
```

```python
import math

import jax
import jax.numpy as jnp
from jax import lax
from jax.sharding import PartitionSpec as P


def cmul(first, second):
    half = first.shape[-1] // 2
    fr = first[..., :half]
    fi = first[..., half:]
    sr = second[..., :half]
    si = second[..., half:]
    return jnp.concatenate([fr * sr - fi * si, fr * si + fi * sr], axis=-1)


def mode_powers(decay_rate, angle, unit, counts):
    phase = jnp.mod(angle * unit, 2.0 * math.pi) * counts
    magnitude = jnp.exp(-decay_rate * unit * counts)
    return jnp.concatenate([magnitude * jnp.cos(phase), magnitude * jnp.sin(phase)], axis=-1)


def radices(count):
    sizes = []
    left = count
    while left > 1:
        size = 4 if left % 4 == 0 else (2 if left % 2 == 0 else left)
        sizes.append(size)
        left = left // size
    return sizes


def carry_in(values, rate_row, angle_row, group, count, reverse):
    unit_one = jnp.ones((1, 1), jnp.float32)

    def shifted(source, span):
        if reverse:
            pairs = [(i + span, i) for i in range(count - span)]
        else:
            pairs = [(i, i + span) for i in range(count - span)]
        return lax.ppermute(source, "tm", pairs)

    if count == 1:
        return jnp.zeros_like(values)
    sizes = radices(count)
    first = min(sizes[0], count - 1)
    acc = shifted(values, 1)
    for step in range(2, first + 1):
        factor = mode_powers(rate_row, angle_row, float(group * (step - 1)), unit_one)
        acc = acc + cmul(factor, shifted(values, step))
    span = first
    for size in sizes[1:]:
        if span >= count - 1:
            break
        moved = acc
        for step in range(1, size):
            if step * span >= count:
                break
            factor = mode_powers(rate_row, angle_row, float(group * span * step), unit_one)
            moved = moved + cmul(factor, shifted(acc, step * span))
        acc = moved
        span = span * size
    return acc


def tm_sum(value, count):
    if count & (count - 1):
        return lax.psum(value, "tm")
    span = 1
    while span < count:
        value = value + lax.ppermute(value, "tm", [(i, i ^ span) for i in range(count)])
        span = span * 2
    return value


def halving_steps(buf, axes, order, count):
    index = lax.axis_index("tm")
    axes = list(axes)
    for bit in order:
        axis = axes.index(bit)
        mine = (index >> bit) & 1
        keep = lax.dynamic_index_in_dim(buf, mine, axis, keepdims=False)
        send = lax.dynamic_index_in_dim(buf, 1 - mine, axis, keepdims=False)
        buf = keep + lax.ppermute(send, "tm", [(i, i ^ (1 << bit)) for i in range(count)])
        axes.pop(axis)
    return buf, axes


def scatter_orders(count):
    depth = count.bit_length() - 1
    return [list(range(depth)), [0, 2, 1] + list(range(3, depth))]


def scatter_begin(pieces, count, lead):
    depth = count.bit_length() - 1
    rows = pieces[0].shape[0] // count
    bufs = []
    for piece, order in zip(pieces, scatter_orders(count)):
        buf = piece.reshape((2,) * depth + (rows, piece.shape[1]))
        bufs.append(halving_steps(buf, range(depth - 1, -1, -1), order[:lead], count)[0])
    return bufs


def column_halves(left, right):
    half = right.shape[2] // 2
    dims = (((0, 1), (0, 1)), ((), ()))
    return [
        lax.dot_general(left, piece, dims, preferred_element_type=jnp.float32)
        for piece in (right[:, :, :half], right[:, :, half:])
    ]


def scatter_finish(bufs, count, lead):
    if count & (count - 1) or count < 4:
        return lax.psum_scatter(bufs, "tm", scatter_dimension=0, tiled=True)
    depth = count.bit_length() - 1
    parts = []
    for buf, order in zip(bufs, scatter_orders(count)):
        axes = [bit for bit in range(depth - 1, -1, -1) if bit not in order[:lead]]
        done = halving_steps(buf, axes, order[lead:], count)[0]
        parts.append(done.reshape(done.shape[-2:]))
    return jnp.concatenate(parts, axis=1)


def per_device(signals, targets, decay_rate, pole_angle, in_map, out_map):
    group = signals.shape[1]
    modes = decay_rate.shape[0]
    width = 2 * modes
    count = lax.axis_size("tm")
    rate_row = decay_rate[None, :]
    fwd_angle = pole_angle[None, :]
    rev_angle = -pole_angle[None, :]
    gain = jnp.sqrt(-jnp.expm1(-2.0 * decay_rate))
    gain_pair = jnp.concatenate([gain, gain])
    unit_one = jnp.ones((1, 1), jnp.float32)
    drive = (
        lax.dot_general(
            signals, in_map, (((2,), (1,)), ((), ())), preferred_element_type=jnp.float32
        )
        * gain_pair
    )
    local = drive
    span = 1
    while span < group:
        factor = mode_powers(rate_row, fwd_angle, float(span), unit_one)
        local = jnp.concatenate(
            [local[:, :span], local[:, span:] + cmul(factor[None], local[:, :-span])], axis=1
        )
        span = span * 2
    ends = local[:, group - 1]
    entering = carry_in(ends, rate_row, fwd_angle, group, count, False)
    offsets = (jnp.arange(group, dtype=jnp.float32) + 1.0)[:, None]
    fwd_table = mode_powers(rate_row, fwd_angle, 1.0, offsets)
    states = local + cmul(fwd_table[None], entering[:, None, :])
    states_b = states.astype(jnp.bfloat16)
    predicted = lax.dot_general(
        states_b, out_map, (((2,), (0,)), ((), ())), preferred_element_type=jnp.float32
    )
    misfit_b = (predicted - targets.astype(jnp.float32)).astype(jnp.bfloat16)
    back = lax.dot_general(
        misfit_b, out_map, (((2,), (1,)), ((), ())), preferred_element_type=jnp.float32
    )
    retro = back
    span = 1
    while span < group:
        factor = mode_powers(rate_row, rev_angle, float(span), unit_one)
        retro = jnp.concatenate(
            [retro[:, :-span] + cmul(factor[None], retro[:, span:]), retro[:, group - span :]],
            axis=1,
        )
        span = span * 2
    starts = retro[:, 0]
    later = carry_in(starts, rate_row, rev_angle, group, count, True)
    remaining = (float(group) - jnp.arange(group, dtype=jnp.float32))[:, None]
    rev_table = mode_powers(rate_row, rev_angle, 1.0, remaining)
    adjoint = retro + cmul(rev_table[None], later[:, None, :])
    scaled = adjoint * gain_pair
    adjoint_b = scaled.astype(jnp.bfloat16)
    boundary_adjoint = scaled[:, 0:1, :]
    if not (count & (count - 1)) and count >= 4:
        out_bufs = scatter_begin(column_halves(states_b, misfit_b), count, 2)
        adjoint_b, out_bufs = lax.optimization_barrier((adjoint_b, out_bufs))
        out_grad = scatter_finish(out_bufs, count, 2)
        in_grad = scatter_finish(
            scatter_begin(column_halves(adjoint_b, signals), count, 0), count, 0
        )
    else:
        out_grad = jnp.concatenate(
            [
                lax.psum_scatter(part, "tm", scatter_dimension=0, tiled=True)
                for part in column_halves(states_b, misfit_b)
            ],
            axis=1,
        )
        in_grad = jnp.concatenate(
            [
                lax.psum_scatter(part, "tm", scatter_dimension=0, tiled=True)
                for part in column_halves(adjoint_b, signals)
            ],
            axis=1,
        )
    out_square = tm_sum(jnp.sum(out_grad * out_grad), count)
    out_update = out_grad * lax.rsqrt(out_square / float(width * out_map.shape[1]) + 1e-06)
    in_square = tm_sum(jnp.sum(in_grad * in_grad), count)
    in_update = in_grad * lax.rsqrt(in_square / float(width * in_map.shape[1]) + 1e-06)
    return (out_update, in_update, boundary_adjoint)


def solution(mesh):
    return jax.shard_map(
        per_device,
        mesh=mesh,
        in_specs=(
            P("grp", "tm", None),
            P("grp", "tm", None),
            P("grp"),
            P("grp"),
            P("grp", None),
            P("grp", None),
        ),
        out_specs=(P(("grp", "tm"), None), P(("grp", "tm"), None), P("grp", "tm", None)),
        check_vma=False,
    )
```

```python
import math

import jax
import jax.numpy as jnp
from jax import lax
from jax.sharding import PartitionSpec as P


def cmul(first, second):
    half = first.shape[-1] // 2
    fr = first[..., :half]
    fi = first[..., half:]
    sr = second[..., :half]
    si = second[..., half:]
    return jnp.concatenate([fr * sr - fi * si, fr * si + fi * sr], axis=-1)


def mode_powers(decay_rate, angle, unit, counts):
    phase = jnp.mod(angle * unit, 2.0 * math.pi) * counts
    magnitude = jnp.exp(-decay_rate * unit * counts)
    return jnp.concatenate([magnitude * jnp.cos(phase), magnitude * jnp.sin(phase)], axis=-1)


def radices(count):
    sizes = []
    left = count
    while left > 1:
        size = 4 if left % 4 == 0 else (2 if left % 2 == 0 else left)
        sizes.append(size)
        left = left // size
    return sizes


def carry_in(values, rate_row, angle_row, group, count, reverse):
    unit_one = jnp.ones((1, 1), jnp.float32)

    def shifted(source, span):
        if reverse:
            pairs = [(i + span, i) for i in range(count - span)]
        else:
            pairs = [(i, i + span) for i in range(count - span)]
        return lax.ppermute(source, "tm", pairs)

    if count == 1:
        return jnp.zeros_like(values)
    sizes = radices(count)
    first = min(sizes[0], count - 1)
    acc = shifted(values, 1)
    for step in range(2, first + 1):
        factor = mode_powers(rate_row, angle_row, float(group * (step - 1)), unit_one)
        acc = acc + cmul(factor, shifted(values, step))
    span = first
    for size in sizes[1:]:
        if span >= count - 1:
            break
        moved = acc
        for step in range(1, size):
            if step * span >= count:
                break
            factor = mode_powers(rate_row, angle_row, float(group * span * step), unit_one)
            moved = moved + cmul(factor, shifted(acc, step * span))
        acc = moved
        span = span * size
    return acc


def tm_sum(value, count):
    if count & (count - 1):
        return lax.psum(value, "tm")
    span = 1
    while span < count:
        value = value + lax.ppermute(value, "tm", [(i, i ^ span) for i in range(count)])
        span = span * 2
    return value


def halving_steps(buf, axes, order, count):
    index = lax.axis_index("tm")
    axes = list(axes)
    for bit in order:
        axis = axes.index(bit)
        mine = (index >> bit) & 1
        keep = lax.dynamic_index_in_dim(buf, mine, axis, keepdims=False)
        send = lax.dynamic_index_in_dim(buf, 1 - mine, axis, keepdims=False)
        buf = keep + lax.ppermute(send, "tm", [(i, i ^ (1 << bit)) for i in range(count)])
        axes.pop(axis)
    return buf, axes


def scatter_orders(count):
    depth = count.bit_length() - 1
    return [list(range(depth)), [0, 2, 1] + list(range(3, depth))]


def scatter_begin(pieces, count, lead):
    depth = count.bit_length() - 1
    rows = pieces[0].shape[0] // count
    bufs = []
    for piece, order in zip(pieces, scatter_orders(count)):
        buf = piece.reshape((2,) * depth + (rows, piece.shape[1]))
        bufs.append(halving_steps(buf, range(depth - 1, -1, -1), order[:lead], count)[0])
    return bufs


def column_halves(left, right):
    half = right.shape[2] // 2
    dims = (((0, 1), (0, 1)), ((), ()))
    return [
        lax.dot_general(left, piece, dims, preferred_element_type=jnp.float32)
        for piece in (right[:, :, :half], right[:, :, half:])
    ]


def scatter_run(bufs, count, begin, end):
    depth = count.bit_length() - 1
    done = []
    for buf, order in zip(bufs, scatter_orders(count)):
        axes = [bit for bit in range(depth - 1, -1, -1) if bit not in order[:begin]]
        done.append(halving_steps(buf, axes, order[begin:end], count)[0])
    return done


def scatter_finish(bufs, count, lead):
    depth = count.bit_length() - 1
    parts = scatter_run(bufs, count, lead, depth)
    return jnp.concatenate([part.reshape(part.shape[-2:]) for part in parts], axis=1)


def per_device(signals, targets, decay_rate, pole_angle, in_map, out_map):
    group = signals.shape[1]
    modes = decay_rate.shape[0]
    width = 2 * modes
    count = lax.axis_size("tm")
    rate_row = decay_rate[None, :]
    fwd_angle = pole_angle[None, :]
    rev_angle = -pole_angle[None, :]
    gain = jnp.sqrt(-jnp.expm1(-2.0 * decay_rate))
    gain_pair = jnp.concatenate([gain, gain])
    unit_one = jnp.ones((1, 1), jnp.float32)
    drive = (
        lax.dot_general(
            signals, in_map, (((2,), (1,)), ((), ())), preferred_element_type=jnp.float32
        )
        * gain_pair
    )
    local = drive
    span = 1
    while span < group:
        factor = mode_powers(rate_row, fwd_angle, float(span), unit_one)
        local = jnp.concatenate(
            [local[:, :span], local[:, span:] + cmul(factor[None], local[:, :-span])], axis=1
        )
        span = span * 2
    ends = local[:, group - 1]
    entering = carry_in(ends, rate_row, fwd_angle, group, count, False)
    offsets = (jnp.arange(group, dtype=jnp.float32) + 1.0)[:, None]
    fwd_table = mode_powers(rate_row, fwd_angle, 1.0, offsets)
    states = local + cmul(fwd_table[None], entering[:, None, :])
    states_b = states.astype(jnp.bfloat16)
    predicted = lax.dot_general(
        states_b, out_map, (((2,), (0,)), ((), ())), preferred_element_type=jnp.float32
    )
    misfit_b = (predicted - targets.astype(jnp.float32)).astype(jnp.bfloat16)
    back = lax.dot_general(
        misfit_b, out_map, (((2,), (1,)), ((), ())), preferred_element_type=jnp.float32
    )
    retro = back
    span = 1
    while span < group:
        factor = mode_powers(rate_row, rev_angle, float(span), unit_one)
        retro = jnp.concatenate(
            [retro[:, :-span] + cmul(factor[None], retro[:, span:]), retro[:, group - span :]],
            axis=1,
        )
        span = span * 2
    starts = retro[:, 0]
    later = carry_in(starts, rate_row, rev_angle, group, count, True)
    remaining = (float(group) - jnp.arange(group, dtype=jnp.float32))[:, None]
    rev_table = mode_powers(rate_row, rev_angle, 1.0, remaining)
    adjoint = retro + cmul(rev_table[None], later[:, None, :])
    scaled = adjoint * gain_pair
    adjoint_b = scaled.astype(jnp.bfloat16)
    boundary_adjoint = scaled[:, 0:1, :]
    if not (count & (count - 1)) and count >= 4:
        out_bufs = scatter_begin(column_halves(states_b, misfit_b), count, 1)
        adjoint_b, out_bufs = lax.optimization_barrier((adjoint_b, out_bufs))
        out_bufs = scatter_run(out_bufs, count, 1, 2)
        in_bufs = scatter_begin(column_halves(adjoint_b, signals), count, 1)
        out_bufs, in_bufs = lax.optimization_barrier((out_bufs, in_bufs))
        out_grad = scatter_finish(out_bufs, count, 2)
        in_grad = scatter_finish(in_bufs, count, 1)
    else:
        out_grad = jnp.concatenate(
            [
                lax.psum_scatter(part, "tm", scatter_dimension=0, tiled=True)
                for part in column_halves(states_b, misfit_b)
            ],
            axis=1,
        )
        in_grad = jnp.concatenate(
            [
                lax.psum_scatter(part, "tm", scatter_dimension=0, tiled=True)
                for part in column_halves(adjoint_b, signals)
            ],
            axis=1,
        )
    out_square = tm_sum(jnp.sum(out_grad * out_grad), count)
    out_update = out_grad * lax.rsqrt(out_square / float(width * out_map.shape[1]) + 1e-06)
    in_square = tm_sum(jnp.sum(in_grad * in_grad), count)
    in_update = in_grad * lax.rsqrt(in_square / float(width * in_map.shape[1]) + 1e-06)
    return (out_update, in_update, boundary_adjoint)


def solution(mesh):
    return jax.shard_map(
        per_device,
        mesh=mesh,
        in_specs=(
            P("grp", "tm", None),
            P("grp", "tm", None),
            P("grp"),
            P("grp"),
            P("grp", None),
            P("grp", None),
        ),
        out_specs=(P(("grp", "tm"), None), P(("grp", "tm"), None), P("grp", "tm", None)),
        check_vma=False,
    )
```

```python
import math

import jax
import jax.numpy as jnp
from jax import lax
from jax.sharding import PartitionSpec as P


def cmul(first, second):
    half = first.shape[-1] // 2
    fr = first[..., :half]
    fi = first[..., half:]
    sr = second[..., :half]
    si = second[..., half:]
    return jnp.concatenate([fr * sr - fi * si, fr * si + fi * sr], axis=-1)


def mode_powers(decay_rate, angle, unit, counts):
    phase = jnp.mod(angle * unit, 2.0 * math.pi) * counts
    magnitude = jnp.exp(-decay_rate * unit * counts)
    return jnp.concatenate([magnitude * jnp.cos(phase), magnitude * jnp.sin(phase)], axis=-1)


def radices(count):
    sizes = []
    left = count
    while left > 1:
        size = 4 if left % 4 == 0 else (2 if left % 2 == 0 else left)
        sizes.append(size)
        left = left // size
    return sizes


def carry_in(values, rate_row, angle_row, group, count, reverse):
    unit_one = jnp.ones((1, 1), jnp.float32)

    def shifted(source, span):
        if reverse:
            pairs = [(i + span, i) for i in range(count - span)]
        else:
            pairs = [(i, i + span) for i in range(count - span)]
        return lax.ppermute(source, "tm", pairs)

    if count == 1:
        return jnp.zeros_like(values)
    sizes = radices(count)
    first = min(sizes[0], count - 1)
    acc = shifted(values, 1)
    for step in range(2, first + 1):
        factor = mode_powers(rate_row, angle_row, float(group * (step - 1)), unit_one)
        acc = acc + cmul(factor, shifted(values, step))
    span = first
    for size in sizes[1:]:
        if span >= count - 1:
            break
        moved = acc
        for step in range(1, size):
            if step * span >= count:
                break
            factor = mode_powers(rate_row, angle_row, float(group * span * step), unit_one)
            moved = moved + cmul(factor, shifted(acc, step * span))
        acc = moved
        span = span * size
    return acc


def tm_sum(value, count):
    if count & (count - 1):
        return lax.psum(value, "tm")
    span = 1
    while span < count:
        value = value + lax.ppermute(value, "tm", [(i, i ^ span) for i in range(count)])
        span = span * 2
    return value


def halving_steps(buf, axes, order, count):
    index = lax.axis_index("tm")
    axes = list(axes)
    for bit in order:
        axis = axes.index(bit)
        mine = (index >> bit) & 1
        keep = lax.dynamic_index_in_dim(buf, mine, axis, keepdims=False)
        send = lax.dynamic_index_in_dim(buf, 1 - mine, axis, keepdims=False)
        buf = keep + lax.ppermute(send, "tm", [(i, i ^ (1 << bit)) for i in range(count)])
        axes.pop(axis)
    return buf, axes


def scatter_orders(count, late=False):
    depth = count.bit_length() - 1
    if late:
        return [list(range(depth)), [0, 1, 3, 2] + list(range(4, depth))]
    return [list(range(depth)), [0, 2, 1] + list(range(3, depth))]


def scatter_begin(pieces, count, lead, late=False):
    depth = count.bit_length() - 1
    rows = pieces[0].shape[0] // count
    bufs = []
    for piece, order in zip(pieces, scatter_orders(count, late)):
        buf = piece.reshape((2,) * depth + (rows, piece.shape[1]))
        bufs.append(halving_steps(buf, range(depth - 1, -1, -1), order[:lead], count)[0])
    return bufs


def column_halves(left, right):
    half = right.shape[2] // 2
    dims = (((0, 1), (0, 1)), ((), ()))
    return [
        lax.dot_general(left, piece, dims, preferred_element_type=jnp.float32)
        for piece in (right[:, :, :half], right[:, :, half:])
    ]


def scatter_finish(bufs, count, lead, late=False):
    if count & (count - 1) or count < 4:
        return lax.psum_scatter(bufs, "tm", scatter_dimension=0, tiled=True)
    depth = count.bit_length() - 1
    parts = []
    for buf, order in zip(bufs, scatter_orders(count, late)):
        axes = [bit for bit in range(depth - 1, -1, -1) if bit not in order[:lead]]
        done = halving_steps(buf, axes, order[lead:], count)[0]
        parts.append(done.reshape(done.shape[-2:]))
    return jnp.concatenate(parts, axis=1)


def per_device(signals, targets, decay_rate, pole_angle, in_map, out_map):
    group = signals.shape[1]
    modes = decay_rate.shape[0]
    width = 2 * modes
    count = lax.axis_size("tm")
    rate_row = decay_rate[None, :]
    fwd_angle = pole_angle[None, :]
    rev_angle = -pole_angle[None, :]
    gain = jnp.sqrt(-jnp.expm1(-2.0 * decay_rate))
    gain_pair = jnp.concatenate([gain, gain])
    unit_one = jnp.ones((1, 1), jnp.float32)
    drive = (
        lax.dot_general(
            signals, in_map, (((2,), (1,)), ((), ())), preferred_element_type=jnp.float32
        )
        * gain_pair
    )
    local = drive
    span = 1
    while span < group:
        factor = mode_powers(rate_row, fwd_angle, float(span), unit_one)
        local = jnp.concatenate(
            [local[:, :span], local[:, span:] + cmul(factor[None], local[:, :-span])], axis=1
        )
        span = span * 2
    ends = local[:, group - 1]
    entering = carry_in(ends, rate_row, fwd_angle, group, count, False)
    offsets = (jnp.arange(group, dtype=jnp.float32) + 1.0)[:, None]
    fwd_table = mode_powers(rate_row, fwd_angle, 1.0, offsets)
    states = local + cmul(fwd_table[None], entering[:, None, :])
    states_b = states.astype(jnp.bfloat16)
    predicted = lax.dot_general(
        states_b, out_map, (((2,), (0,)), ((), ())), preferred_element_type=jnp.float32
    )
    misfit_b = (predicted - targets.astype(jnp.float32)).astype(jnp.bfloat16)
    back = lax.dot_general(
        misfit_b, out_map, (((2,), (1,)), ((), ())), preferred_element_type=jnp.float32
    )
    retro = back
    span = 1
    while span < group:
        factor = mode_powers(rate_row, rev_angle, float(span), unit_one)
        retro = jnp.concatenate(
            [retro[:, :-span] + cmul(factor[None], retro[:, span:]), retro[:, group - span :]],
            axis=1,
        )
        span = span * 2
    starts = retro[:, 0]
    later = carry_in(starts, rate_row, rev_angle, group, count, True)
    remaining = (float(group) - jnp.arange(group, dtype=jnp.float32))[:, None]
    rev_table = mode_powers(rate_row, rev_angle, 1.0, remaining)
    adjoint = retro + cmul(rev_table[None], later[:, None, :])
    scaled = adjoint * gain_pair
    adjoint_b = scaled.astype(jnp.bfloat16)
    boundary_adjoint = scaled[:, 0:1, :]
    if not (count & (count - 1)) and count >= 4:
        out_bufs = scatter_begin(column_halves(states_b, misfit_b), count, 2)
        adjoint_b, out_bufs = lax.optimization_barrier((adjoint_b, out_bufs))
        out_grad = scatter_finish(out_bufs, count, 2)
        in_grad = scatter_finish(
            scatter_begin(column_halves(adjoint_b, signals), count, 0, True), count, 0, True
        )
    else:
        out_grad = jnp.concatenate(
            [
                lax.psum_scatter(part, "tm", scatter_dimension=0, tiled=True)
                for part in column_halves(states_b, misfit_b)
            ],
            axis=1,
        )
        in_grad = jnp.concatenate(
            [
                lax.psum_scatter(part, "tm", scatter_dimension=0, tiled=True)
                for part in column_halves(adjoint_b, signals)
            ],
            axis=1,
        )
    out_square = tm_sum(jnp.sum(out_grad * out_grad), count)
    out_update = out_grad * lax.rsqrt(out_square / float(width * out_map.shape[1]) + 1e-06)
    in_square = tm_sum(jnp.sum(in_grad * in_grad), count)
    in_update = in_grad * lax.rsqrt(in_square / float(width * in_map.shape[1]) + 1e-06)
    return (out_update, in_update, boundary_adjoint)


def solution(mesh):
    return jax.shard_map(
        per_device,
        mesh=mesh,
        in_specs=(
            P("grp", "tm", None),
            P("grp", "tm", None),
            P("grp"),
            P("grp"),
            P("grp", None),
            P("grp", None),
        ),
        out_specs=(P(("grp", "tm"), None), P(("grp", "tm"), None), P("grp", "tm", None)),
        check_vma=False,
    )
```

```python
import math

import jax
import jax.numpy as jnp
from jax import lax
from jax.sharding import PartitionSpec as P


def cmul(first, second):
    half = first.shape[-1] // 2
    fr = first[..., :half]
    fi = first[..., half:]
    sr = second[..., :half]
    si = second[..., half:]
    return jnp.concatenate([fr * sr - fi * si, fr * si + fi * sr], axis=-1)


def mode_powers(decay_rate, angle, unit, counts):
    phase = jnp.mod(angle * unit, 2.0 * math.pi) * counts
    magnitude = jnp.exp(-decay_rate * unit * counts)
    return jnp.concatenate([magnitude * jnp.cos(phase), magnitude * jnp.sin(phase)], axis=-1)


def radices(count):
    sizes = []
    left = count
    while left > 1:
        size = 4 if left % 4 == 0 else (2 if left % 2 == 0 else left)
        sizes.append(size)
        left = left // size
    return sizes


def carry_in(values, rate_row, angle_row, group, count, reverse):
    unit_one = jnp.ones((1, 1), jnp.float32)

    def shifted(source, span):
        if reverse:
            pairs = [(i + span, i) for i in range(count - span)]
        else:
            pairs = [(i, i + span) for i in range(count - span)]
        return lax.ppermute(source, "tm", pairs)

    if count == 1:
        return jnp.zeros_like(values)
    sizes = radices(count)
    first = min(sizes[0], count - 1)
    acc = shifted(values, 1)
    for step in range(2, first + 1):
        factor = mode_powers(rate_row, angle_row, float(group * (step - 1)), unit_one)
        acc = acc + cmul(factor, shifted(values, step))
    span = first
    for size in sizes[1:]:
        if span >= count - 1:
            break
        moved = acc
        for step in range(1, size):
            if step * span >= count:
                break
            factor = mode_powers(rate_row, angle_row, float(group * span * step), unit_one)
            moved = moved + cmul(factor, shifted(acc, step * span))
        acc = moved
        span = span * size
    return acc


def tm_sum(value, count):
    if count & (count - 1):
        return lax.psum(value, "tm")
    span = 1
    while span < count:
        value = value + lax.ppermute(value, "tm", [(i, i ^ span) for i in range(count)])
        span = span * 2
    return value


def halving_steps(buf, axes, order, count):
    index = lax.axis_index("tm")
    axes = list(axes)
    for bit in order:
        axis = axes.index(bit)
        mine = (index >> bit) & 1
        keep = lax.dynamic_index_in_dim(buf, mine, axis, keepdims=False)
        send = lax.dynamic_index_in_dim(buf, 1 - mine, axis, keepdims=False)
        buf = keep + lax.ppermute(send, "tm", [(i, i ^ (1 << bit)) for i in range(count)])
        axes.pop(axis)
    return buf, axes


def scatter_orders(count):
    depth = count.bit_length() - 1
    return [list(range(depth)), [0, 2, 1] + list(range(3, depth))]


def scatter_begin(pieces, count, lead):
    depth = count.bit_length() - 1
    rows = pieces[0].shape[0] // count
    bufs = []
    for piece, order in zip(pieces, scatter_orders(count)):
        buf = piece.reshape((2,) * depth + (rows, piece.shape[1]))
        bufs.append(halving_steps(buf, range(depth - 1, -1, -1), order[:lead], count)[0])
    return bufs


def column_halves(left, right):
    half = right.shape[2] // 2
    dims = (((0, 1), (0, 1)), ((), ()))
    return [
        lax.dot_general(left, piece, dims, preferred_element_type=jnp.float32)
        for piece in (right[:, :, :half], right[:, :, half:])
    ]


def scatter_finish(bufs, count, lead):
    if count & (count - 1) or count < 4:
        return lax.psum_scatter(bufs, "tm", scatter_dimension=0, tiled=True)
    depth = count.bit_length() - 1
    parts = []
    for buf, order in zip(bufs, scatter_orders(count)):
        axes = [bit for bit in range(depth - 1, -1, -1) if bit not in order[:lead]]
        done = halving_steps(buf, axes, order[lead:], count)[0]
        parts.append(done.reshape(done.shape[-2:]))
    return jnp.concatenate(parts, axis=1)


def per_device(signals, targets, decay_rate, pole_angle, in_map, out_map):
    group = signals.shape[1]
    modes = decay_rate.shape[0]
    width = 2 * modes
    count = lax.axis_size("tm")
    rate_row = decay_rate[None, :]
    fwd_angle = pole_angle[None, :]
    rev_angle = -pole_angle[None, :]
    gain = jnp.sqrt(-jnp.expm1(-2.0 * decay_rate))
    gain_pair = jnp.concatenate([gain, gain])
    unit_one = jnp.ones((1, 1), jnp.float32)
    drive = (
        lax.dot_general(
            signals, in_map, (((2,), (1,)), ((), ())), preferred_element_type=jnp.float32
        )
        * gain_pair
    )
    local = drive
    span = 1
    while span < group:
        factor = mode_powers(rate_row, fwd_angle, float(span), unit_one)
        local = local + jnp.pad(
            cmul(factor[None], local[:, :-span]), ((0, 0), (span, 0), (0, 0))
        )
        span = span * 2
    ends = local[:, group - 1]
    entering = carry_in(ends, rate_row, fwd_angle, group, count, False)
    offsets = (jnp.arange(group, dtype=jnp.float32) + 1.0)[:, None]
    fwd_table = mode_powers(rate_row, fwd_angle, 1.0, offsets)
    states = local + cmul(fwd_table[None], entering[:, None, :])
    states_b = states.astype(jnp.bfloat16)
    predicted = lax.dot_general(
        states_b, out_map, (((2,), (0,)), ((), ())), preferred_element_type=jnp.float32
    )
    misfit_b = (predicted - targets.astype(jnp.float32)).astype(jnp.bfloat16)
    back = lax.dot_general(
        misfit_b, out_map, (((2,), (1,)), ((), ())), preferred_element_type=jnp.float32
    )
    retro = back
    span = 1
    while span < group:
        factor = mode_powers(rate_row, rev_angle, float(span), unit_one)
        retro = retro + jnp.pad(
            cmul(factor[None], retro[:, span:]), ((0, 0), (0, span), (0, 0))
        )
        span = span * 2
    starts = retro[:, 0]
    later = carry_in(starts, rate_row, rev_angle, group, count, True)
    remaining = (float(group) - jnp.arange(group, dtype=jnp.float32))[:, None]
    rev_table = mode_powers(rate_row, rev_angle, 1.0, remaining)
    adjoint = retro + cmul(rev_table[None], later[:, None, :])
    scaled = adjoint * gain_pair
    adjoint_b = scaled.astype(jnp.bfloat16)
    boundary_adjoint = scaled[:, 0:1, :]
    if not (count & (count - 1)) and count >= 4:
        out_bufs = scatter_begin(column_halves(states_b, misfit_b), count, 2)
        adjoint_b, out_bufs = lax.optimization_barrier((adjoint_b, out_bufs))
        out_grad = scatter_finish(out_bufs, count, 2)
        in_grad = scatter_finish(
            scatter_begin(column_halves(adjoint_b, signals), count, 0), count, 0
        )
    else:
        out_grad = jnp.concatenate(
            [
                lax.psum_scatter(part, "tm", scatter_dimension=0, tiled=True)
                for part in column_halves(states_b, misfit_b)
            ],
            axis=1,
        )
        in_grad = jnp.concatenate(
            [
                lax.psum_scatter(part, "tm", scatter_dimension=0, tiled=True)
                for part in column_halves(adjoint_b, signals)
            ],
            axis=1,
        )
    out_square = tm_sum(jnp.sum(out_grad * out_grad), count)
    out_update = out_grad * lax.rsqrt(out_square / float(width * out_map.shape[1]) + 1e-06)
    in_square = tm_sum(jnp.sum(in_grad * in_grad), count)
    in_update = in_grad * lax.rsqrt(in_square / float(width * in_map.shape[1]) + 1e-06)
    return (out_update, in_update, boundary_adjoint)


def solution(mesh):
    return jax.shard_map(
        per_device,
        mesh=mesh,
        in_specs=(
            P("grp", "tm", None),
            P("grp", "tm", None),
            P("grp"),
            P("grp"),
            P("grp", None),
            P("grp", None),
        ),
        out_specs=(P(("grp", "tm"), None), P(("grp", "tm"), None), P("grp", "tm", None)),
        check_vma=False,
    )
```

```python
import math

import jax
import jax.numpy as jnp
from jax import lax
from jax.sharding import PartitionSpec as P


def cmul(first, second):
    half = first.shape[-1] // 2
    fr = first[..., :half]
    fi = first[..., half:]
    sr = second[..., :half]
    si = second[..., half:]
    return jnp.concatenate([fr * sr - fi * si, fr * si + fi * sr], axis=-1)


def mode_powers(decay_rate, angle, unit, counts):
    phase = jnp.mod(angle * unit, 2.0 * math.pi) * counts
    magnitude = jnp.exp(-decay_rate * unit * counts)
    return jnp.concatenate([magnitude * jnp.cos(phase), magnitude * jnp.sin(phase)], axis=-1)


def radices(count):
    sizes = []
    left = count
    while left > 1:
        size = 4 if left % 4 == 0 else (2 if left % 2 == 0 else left)
        sizes.append(size)
        left = left // size
    return sizes


def carry_in(values, rate_row, angle_row, group, count, reverse):
    unit_one = jnp.ones((1, 1), jnp.float32)

    def shifted(source, span):
        if reverse:
            pairs = [(i + span, i) for i in range(count - span)]
        else:
            pairs = [(i, i + span) for i in range(count - span)]
        return lax.ppermute(source, "tm", pairs)

    if count == 1:
        return jnp.zeros_like(values)
    sizes = radices(count)
    first = min(sizes[0], count - 1)
    acc = shifted(values, 1)
    for step in range(2, first + 1):
        factor = mode_powers(rate_row, angle_row, float(group * (step - 1)), unit_one)
        acc = acc + cmul(factor, shifted(values, step))
    span = first
    for size in sizes[1:]:
        if span >= count - 1:
            break
        moved = acc
        for step in range(1, size):
            if step * span >= count:
                break
            factor = mode_powers(rate_row, angle_row, float(group * span * step), unit_one)
            moved = moved + cmul(factor, shifted(acc, step * span))
        acc = moved
        span = span * size
    return acc


def tm_sum(value, count):
    if count & (count - 1):
        return lax.psum(value, "tm")
    span = 1
    while span < count:
        value = value + lax.ppermute(value, "tm", [(i, i ^ span) for i in range(count)])
        span = span * 2
    return value


def halving_steps(buf, axes, order, count):
    index = lax.axis_index("tm")
    axes = list(axes)
    for bit in order:
        axis = axes.index(bit)
        mine = (index >> bit) & 1
        keep = lax.dynamic_index_in_dim(buf, mine, axis, keepdims=False)
        send = lax.dynamic_index_in_dim(buf, 1 - mine, axis, keepdims=False)
        buf = keep + lax.ppermute(send, "tm", [(i, i ^ (1 << bit)) for i in range(count)])
        axes.pop(axis)
    return buf, axes


def scatter_orders(count):
    depth = count.bit_length() - 1
    return [list(range(depth)), [0, 2, 1] + list(range(3, depth))]


def scatter_begin(pieces, count, lead):
    depth = count.bit_length() - 1
    rows = pieces[0].shape[0] // count
    bufs = []
    for piece, order in zip(pieces, scatter_orders(count)):
        buf = piece.reshape((2,) * depth + (rows, piece.shape[1]))
        axes = [0] + list(range(depth - 1, 0, -1))
        bufs.append(halving_steps(buf, axes, order[:lead], count)[0])
    return bufs


def column_halves(left, right):
    members, steps, width = left.shape
    block = width // lax.axis_size("tm")
    left = left.reshape(members, steps, width // (2 * block), 2, block)
    left = left.transpose(0, 1, 3, 2, 4).reshape(members, steps, width)
    half = right.shape[2] // 2
    dims = (((0, 1), (0, 1)), ((), ()))
    return [
        lax.dot_general(left, piece, dims, preferred_element_type=jnp.float32)
        for piece in (right[:, :, :half], right[:, :, half:])
    ]


def plain_halves(left, right):
    half = right.shape[2] // 2
    dims = (((0, 1), (0, 1)), ((), ()))
    return [
        lax.dot_general(left, piece, dims, preferred_element_type=jnp.float32)
        for piece in (right[:, :, :half], right[:, :, half:])
    ]


def scatter_finish(bufs, count, lead):
    if count & (count - 1) or count < 4:
        return lax.psum_scatter(bufs, "tm", scatter_dimension=0, tiled=True)
    depth = count.bit_length() - 1
    parts = []
    for buf, order in zip(bufs, scatter_orders(count)):
        axes = [bit for bit in range(depth - 1, -1, -1) if bit not in order[:lead]]
        done = halving_steps(buf, axes, order[lead:], count)[0]
        parts.append(done.reshape(done.shape[-2:]))
    return jnp.concatenate(parts, axis=1)


def per_device(signals, targets, decay_rate, pole_angle, in_map, out_map):
    group = signals.shape[1]
    modes = decay_rate.shape[0]
    width = 2 * modes
    count = lax.axis_size("tm")
    rate_row = decay_rate[None, :]
    fwd_angle = pole_angle[None, :]
    rev_angle = -pole_angle[None, :]
    gain = jnp.sqrt(-jnp.expm1(-2.0 * decay_rate))
    gain_pair = jnp.concatenate([gain, gain])
    unit_one = jnp.ones((1, 1), jnp.float32)
    drive = (
        lax.dot_general(
            signals, in_map, (((2,), (1,)), ((), ())), preferred_element_type=jnp.float32
        )
        * gain_pair
    )
    local = drive
    span = 1
    while span < group:
        factor = mode_powers(rate_row, fwd_angle, float(span), unit_one)
        local = jnp.concatenate(
            [local[:, :span], local[:, span:] + cmul(factor[None], local[:, :-span])], axis=1
        )
        span = span * 2
    ends = local[:, group - 1]
    entering = carry_in(ends, rate_row, fwd_angle, group, count, False)
    offsets = (jnp.arange(group, dtype=jnp.float32) + 1.0)[:, None]
    fwd_table = mode_powers(rate_row, fwd_angle, 1.0, offsets)
    states = local + cmul(fwd_table[None], entering[:, None, :])
    states_b = states.astype(jnp.bfloat16)
    predicted = lax.dot_general(
        states_b, out_map, (((2,), (0,)), ((), ())), preferred_element_type=jnp.float32
    )
    misfit_b = (predicted - targets.astype(jnp.float32)).astype(jnp.bfloat16)
    back = lax.dot_general(
        misfit_b, out_map, (((2,), (1,)), ((), ())), preferred_element_type=jnp.float32
    )
    retro = back
    span = 1
    while span < group:
        factor = mode_powers(rate_row, rev_angle, float(span), unit_one)
        retro = jnp.concatenate(
            [retro[:, :-span] + cmul(factor[None], retro[:, span:]), retro[:, group - span :]],
            axis=1,
        )
        span = span * 2
    starts = retro[:, 0]
    later = carry_in(starts, rate_row, rev_angle, group, count, True)
    remaining = (float(group) - jnp.arange(group, dtype=jnp.float32))[:, None]
    rev_table = mode_powers(rate_row, rev_angle, 1.0, remaining)
    adjoint = retro + cmul(rev_table[None], later[:, None, :])
    scaled = adjoint * gain_pair
    adjoint_b = scaled.astype(jnp.bfloat16)
    boundary_adjoint = scaled[:, 0:1, :]
    if not (count & (count - 1)) and count >= 4:
        out_bufs = scatter_begin(column_halves(states_b, misfit_b), count, 2)
        adjoint_b, out_bufs = lax.optimization_barrier((adjoint_b, out_bufs))
        out_grad = scatter_finish(out_bufs, count, 2)
        in_grad = scatter_finish(
            scatter_begin(column_halves(adjoint_b, signals), count, 1), count, 1
        )
    else:
        out_grad = jnp.concatenate(
            [
                lax.psum_scatter(part, "tm", scatter_dimension=0, tiled=True)
                for part in plain_halves(states_b, misfit_b)
            ],
            axis=1,
        )
        in_grad = jnp.concatenate(
            [
                lax.psum_scatter(part, "tm", scatter_dimension=0, tiled=True)
                for part in plain_halves(adjoint_b, signals)
            ],
            axis=1,
        )
    out_square = tm_sum(jnp.sum(out_grad * out_grad), count)
    out_update = out_grad * lax.rsqrt(out_square / float(width * out_map.shape[1]) + 1e-06)
    in_square = tm_sum(jnp.sum(in_grad * in_grad), count)
    in_update = in_grad * lax.rsqrt(in_square / float(width * in_map.shape[1]) + 1e-06)
    return (out_update, in_update, boundary_adjoint)


def solution(mesh):
    return jax.shard_map(
        per_device,
        mesh=mesh,
        in_specs=(
            P("grp", "tm", None),
            P("grp", "tm", None),
            P("grp"),
            P("grp"),
            P("grp", None),
            P("grp", None),
        ),
        out_specs=(P(("grp", "tm"), None), P(("grp", "tm"), None), P("grp", "tm", None)),
        check_vma=False,
    )
```

```python
import math

import jax
import jax.numpy as jnp
from jax import lax
from jax.sharding import PartitionSpec as P


def cmul(first, second):
    half = first.shape[-1] // 2
    fr = first[..., :half]
    fi = first[..., half:]
    sr = second[..., :half]
    si = second[..., half:]
    return jnp.concatenate([fr * sr - fi * si, fr * si + fi * sr], axis=-1)


def mode_powers(decay_rate, angle, unit, counts):
    phase = jnp.mod(angle * unit, 2.0 * math.pi) * counts
    magnitude = jnp.exp(-decay_rate * unit * counts)
    return jnp.concatenate([magnitude * jnp.cos(phase), magnitude * jnp.sin(phase)], axis=-1)


def radices(count):
    sizes = []
    left = count
    while left > 1:
        size = 4 if left % 4 == 0 else (2 if left % 2 == 0 else left)
        sizes.append(size)
        left = left // size
    return sizes


def carry_in(values, rate_row, angle_row, group, count, reverse):
    unit_one = jnp.ones((1, 1), jnp.float32)

    def shifted(source, span):
        if reverse:
            pairs = [(i + span, i) for i in range(count - span)]
        else:
            pairs = [(i, i + span) for i in range(count - span)]
        return lax.ppermute(source, "tm", pairs)

    if count == 1:
        return jnp.zeros_like(values)
    sizes = radices(count)
    first = min(sizes[0], count - 1)
    acc = shifted(values, 1)
    for step in range(2, first + 1):
        factor = mode_powers(rate_row, angle_row, float(group * (step - 1)), unit_one)
        acc = acc + cmul(factor, shifted(values, step))
    span = first
    for size in sizes[1:]:
        if span >= count - 1:
            break
        moved = acc
        for step in range(1, size):
            if step * span >= count:
                break
            factor = mode_powers(rate_row, angle_row, float(group * span * step), unit_one)
            moved = moved + cmul(factor, shifted(acc, step * span))
        acc = moved
        span = span * size
    return acc


def tm_sum(value, count):
    if count & (count - 1):
        return lax.psum(value, "tm")
    span = 1
    while span < count:
        value = value + lax.ppermute(value, "tm", [(i, i ^ span) for i in range(count)])
        span = span * 2
    return value


def halving_steps(buf, axes, order, count):
    index = lax.axis_index("tm")
    axes = list(axes)
    for bit in order:
        axis = axes.index(bit)
        mine = (index >> bit) & 1
        keep = lax.dynamic_index_in_dim(buf, mine, axis, keepdims=False)
        send = lax.dynamic_index_in_dim(buf, 1 - mine, axis, keepdims=False)
        buf = keep + lax.ppermute(send, "tm", [(i, i ^ (1 << bit)) for i in range(count)])
        axes.pop(axis)
    return buf, axes


def scatter_orders(count):
    depth = count.bit_length() - 1
    return [list(range(depth)), [0, 2, 1] + list(range(3, depth))]


def scatter_begin(pieces, count, lead):
    depth = count.bit_length() - 1
    rows = pieces[0].shape[0] // count
    bufs = []
    for piece, order in zip(pieces, scatter_orders(count)):
        buf = piece.reshape((2,) * depth + (rows, piece.shape[1]))
        bufs.append(halving_steps(buf, range(depth - 1, -1, -1), order[:lead], count)[0])
    return bufs


def column_halves(left, right):
    half = right.shape[2] // 2
    dims = (((0, 1), (0, 1)), ((), ()))
    return [
        lax.dot_general(left, piece, dims, preferred_element_type=jnp.float32)
        for piece in (right[:, :, :half], right[:, :, half:])
    ]


def scatter_finish(bufs, count, lead):
    if count & (count - 1) or count < 4:
        return lax.psum_scatter(bufs, "tm", scatter_dimension=0, tiled=True)
    depth = count.bit_length() - 1
    parts = []
    for buf, order in zip(bufs, scatter_orders(count)):
        axes = [bit for bit in range(depth - 1, -1, -1) if bit not in order[:lead]]
        done = halving_steps(buf, axes, order[lead:], count)[0]
        parts.append(done.reshape(done.shape[-2:]))
    return jnp.concatenate(parts, axis=1)


def per_device(signals, targets, decay_rate, pole_angle, in_map, out_map):
    group = signals.shape[1]
    modes = decay_rate.shape[0]
    width = 2 * modes
    count = lax.axis_size("tm")
    rate_row = decay_rate[None, :]
    fwd_angle = pole_angle[None, :]
    rev_angle = -pole_angle[None, :]
    gain = jnp.sqrt(-jnp.expm1(-2.0 * decay_rate))
    gain_pair = jnp.concatenate([gain, gain])
    unit_one = jnp.ones((1, 1), jnp.float32)
    drive = (
        lax.dot_general(
            signals, in_map, (((2,), (1,)), ((), ())), preferred_element_type=jnp.float32
        )
        * gain_pair
    )
    local = drive
    span = 1
    while span < group:
        factor = mode_powers(rate_row, fwd_angle, float(span), unit_one)
        local = jnp.concatenate(
            [local[:, :span], local[:, span:] + cmul(factor[None], local[:, :-span])], axis=1
        )
        span = span * 2
    ends = local[:, group - 1]
    entering = carry_in(ends, rate_row, fwd_angle, group, count, False)
    offsets = (jnp.arange(group, dtype=jnp.float32) + 1.0)[:, None]
    fwd_table = mode_powers(rate_row, fwd_angle, 1.0, offsets)
    states = local + cmul(fwd_table[None], entering[:, None, :])
    states_b = states.astype(jnp.bfloat16)
    predicted = lax.dot_general(
        states_b, out_map, (((2,), (0,)), ((), ())), preferred_element_type=jnp.float32
    )
    misfit_b = (predicted - targets.astype(jnp.float32)).astype(jnp.bfloat16)
    back = lax.dot_general(
        misfit_b, out_map, (((2,), (1,)), ((), ())), preferred_element_type=jnp.float32
    )
    retro = back
    span = 1
    while span < group:
        factor = mode_powers(rate_row, rev_angle, float(span), unit_one)
        retro = jnp.concatenate(
            [retro[:, :-span] + cmul(factor[None], retro[:, span:]), retro[:, group - span :]],
            axis=1,
        )
        span = span * 2
    starts = retro[:, 0]
    later = carry_in(starts, rate_row, rev_angle, group, count, True)
    remaining = (float(group) - jnp.arange(group, dtype=jnp.float32))[:, None]
    rev_table = mode_powers(rate_row, rev_angle, 1.0, remaining)
    adjoint = retro + cmul(rev_table[None], later[:, None, :])
    scaled = adjoint * gain_pair
    adjoint_b = scaled.astype(jnp.bfloat16)
    boundary_adjoint = scaled[:, 0:1, :]
    if not (count & (count - 1)) and count >= 4:
        out_bufs = scatter_begin(column_halves(states_b, misfit_b), count, 2)
        adjoint_b, out_bufs = lax.optimization_barrier((adjoint_b, out_bufs))
        out_grad = scatter_finish(out_bufs, count, 2)
        in_grad = scatter_finish(
            scatter_begin(column_halves(adjoint_b, signals), count, 0), count, 0
        )
    else:
        out_grad = jnp.concatenate(
            [
                lax.psum_scatter(part, "tm", scatter_dimension=0, tiled=True)
                for part in column_halves(states_b, misfit_b)
            ],
            axis=1,
        )
        in_grad = jnp.concatenate(
            [
                lax.psum_scatter(part, "tm", scatter_dimension=0, tiled=True)
                for part in column_halves(adjoint_b, signals)
            ],
            axis=1,
        )
    squares = tm_sum(jnp.stack([jnp.sum(out_grad * out_grad), jnp.sum(in_grad * in_grad)]), count)
    out_update = out_grad * lax.rsqrt(squares[0] / float(width * out_map.shape[1]) + 1e-06)
    in_update = in_grad * lax.rsqrt(squares[1] / float(width * in_map.shape[1]) + 1e-06)
    return (out_update, in_update, boundary_adjoint)


def solution(mesh):
    return jax.shard_map(
        per_device,
        mesh=mesh,
        in_specs=(
            P("grp", "tm", None),
            P("grp", "tm", None),
            P("grp"),
            P("grp"),
            P("grp", None),
            P("grp", None),
        ),
        out_specs=(P(("grp", "tm"), None), P(("grp", "tm"), None), P("grp", "tm", None)),
        check_vma=False,
    )
```
